32 devices in a mesh: grp: 2 (over x), blk: 16 (over z, y, core).
Axes of the slice: x: 2, y: 2, z: 4, core: 2. Of those that a mesh axis runs over, the one named last changes fastest.
Arguments:
- queries: bfloat16 [512, 2048], P(('grp', 'blk')), parts along dimension 0, may hold values from 0 to 2, as said below
- library: bfloat16 [24576, 2048], P(('grp', 'blk')), parts along dimension 0, may hold values from 0 to 2, as said below
- assays: bfloat16 [24576, 256], P(('grp', 'blk')), parts along dimension 0, may hold values from -14 to 14
Outputs:
- smoothed: float32 [512, 256], P(('grp', 'blk')), parts along dimension 0
The draws below stay inside these ranges and needn't reach their ends.
There are 2 independent parts, one for each index of `grp`. The reference program is written for one: setup_inputs(seed, part) draws one part's arguments, and reference() takes and returns one part's arrays. A program takes and returns all parts, laid end to end along the dimension named above; each array names one. Nothing has to cross between parts.
Inputs may be any that keep to these rules, and one draw needn't show every extreme that they name: `queries`: nonnegative fingerprint features. `library`: nonnegative fingerprint features.
All inputs are finite; a program needn't handle non-finite values.
Results may differ from the reference program's by a relative error of at most 0.002.
Values may be sent and summed in bfloat16 or wider, within the bound.
No kernel may reach another device: no remote copies, remote signals or barrier semaphores. Data moves between devices by JAX's collectives and lax.ppermute only.
A program may use at most 64 MiB of HBM per device.

```python
import jax
import jax.numpy as jnp
from jax import lax

F = 2048
A = 256
Q_DEV = 16
QUERIES = 256
LIBRARY = 12288
N_BLK = 16


def cluster_tables(key):
    clusters = LIBRARY // 16
    proto = jax.random.uniform(jax.random.fold_in(key, 11), (clusters, F)) ** 3
    lib_ids = jax.random.randint(jax.random.fold_in(key, 12), (LIBRARY,), 0, clusters)
    query_ids = jax.random.randint(jax.random.fold_in(key, 13), (QUERIES,), 0, clusters)
    return (proto, lib_ids, query_ids)


def draw_queries(key, part):
    proto, lib_ids, query_ids = cluster_tables(key)
    base = jnp.take(proto, query_ids, axis=0)
    level = jax.random.uniform(jax.random.fold_in(key, 21), (QUERIES, 1), minval=0.2, maxval=0.8)
    noise = jax.random.uniform(jax.random.fold_in(key, 22), (QUERIES, F)) ** 3
    return (base + level * noise).astype(jnp.bfloat16)


def draw_library(key, part):
    proto, lib_ids, query_ids = cluster_tables(key)
    base = jnp.take(proto, lib_ids, axis=0)
    level = jax.random.uniform(jax.random.fold_in(key, 31), (LIBRARY, 1), minval=0.2, maxval=0.8)
    noise = jax.random.uniform(jax.random.fold_in(key, 32), (LIBRARY, F)) ** 3
    return (base + level * noise).astype(jnp.bfloat16)


def draw_assays(key, part):
    proto, lib_ids, query_ids = cluster_tables(key)
    clusters = LIBRARY // 16
    value_proto = jax.random.uniform(jax.random.fold_in(key, 14), (clusters, A), minval=-2.0, maxval=2.0)
    offset = jax.random.uniform(jax.random.fold_in(key, 15), (A,), minval=-1.0, maxval=1.0)
    position = jnp.arange(LIBRARY, dtype=jnp.float32)[:, None] / LIBRARY
    noise = jnp.clip(jax.random.normal(jax.random.fold_in(key, 41), (LIBRARY, A)), -3.0, 3.0)
    scale = 1.0 + 2.0 * position
    values = (jnp.take(value_proto, lib_ids, axis=0) + 0.7 * noise) * scale + offset
    return values.astype(jnp.bfloat16)


def setup_inputs(seed: int = 0, part: int = 0) -> dict:
    arg_keys = jax.random.split(jax.random.key(seed), 4)
    own_keys = jax.random.split(jax.random.fold_in(arg_keys[3], part), 4)
    return {
        "queries": draw_queries(jax.random.fold_in(jax.random.fold_in(arg_keys[3], part), 71), part),
        "library": draw_library(jax.random.fold_in(jax.random.fold_in(arg_keys[3], part), 71), part),
        "assays": draw_assays(jax.random.fold_in(jax.random.fold_in(arg_keys[3], part), 71), part),
    }


EPS = 1e-05
TAU = 0.05

def reference(queries, library, assays):
    values = assays.astype(jnp.float32)
    mean = lax.optimization_barrier(jnp.mean(values, axis=0))
    spread = lax.optimization_barrier(jnp.mean(values * values, axis=0)) - mean * mean
    zvals = ((values - mean) * lax.rsqrt(spread + EPS)).astype(jnp.bfloat16)
    libf = library.astype(jnp.float32)
    lib_sq = lax.optimization_barrier(jnp.sum(libf * libf, axis=1))
    zvalf = zvals.astype(jnp.float32)
    blocks = queries.reshape(N_BLK, Q_DEV, F)

    def one_block(block):
        blockf = block.astype(jnp.float32)
        q_sq = lax.optimization_barrier(jnp.sum(blockf * blockf, axis=1))
        inner = jnp.dot(blockf, libf.T, precision=lax.Precision.HIGHEST)
        tanimoto = inner / (q_sq[:, None] + lib_sq[None, :] - inner)
        weight = jnp.exp((tanimoto - 1.0) / TAU)
        weight_b = weight.astype(jnp.bfloat16).astype(jnp.float32)
        numer = jnp.dot(weight_b, zvalf, precision=lax.Precision.HIGHEST)
        denom = lax.optimization_barrier(jnp.sum(weight, axis=1))
        return numer / denom[:, None]
    return lax.map(one_block, blocks).reshape(QUERIES, A)
```

```python
import jax
import jax.numpy as jnp
from jax import lax
from jax.sharding import PartitionSpec as P

EPS = 1e-05
TAU = 0.05


def split3(x):
    hi = x.astype(jnp.bfloat16)
    rest = x - hi.astype(jnp.float32)
    mid = rest.astype(jnp.bfloat16)
    lo = (rest - mid.astype(jnp.float32)).astype(jnp.bfloat16)
    return jnp.concatenate([hi, mid, lo])


def join3(parts, n):
    parts = parts.astype(jnp.float32)
    return (parts[..., :n] + parts[..., n:2 * n]) + parts[..., 2 * n:3 * n]


def weighted_sums(block, library, lib_sq, zvals):
    blockf = block.astype(jnp.float32)
    q_sq = jnp.sum(blockf * blockf, axis=1)
    inner = lax.dot_general(
        block, library, (((1,), (1,)), ((), ())), preferred_element_type=jnp.float32
    )
    tanimoto = inner / (q_sq[:, None] + lib_sq[None, :] - inner)
    weight = jnp.exp((tanimoto - 1.0) / TAU)
    numer = jnp.dot(weight.astype(jnp.bfloat16), zvals, preferred_element_type=jnp.float32)
    denom = jnp.sum(weight, axis=1)
    return (numer, denom)


def shards(queries, library, assays):
    nblk = lax.axis_size("blk")
    q_dev, feat = queries.shape
    width = assays.shape[1]
    values = assays.astype(jnp.float32)
    partial = jnp.concatenate([jnp.sum(values, axis=0), jnp.sum(values * values, axis=0)])
    coded = split3(partial)
    stat_rows = -(-coded.shape[0] // feat)
    coded = jnp.pad(coded, (0, stat_rows * feat - coded.shape[0])).reshape(stat_rows, feat)

    packet = jnp.concatenate([queries, coded], axis=0)
    gathered = lax.all_gather(packet, "blk", tiled=False)
    everyone = gathered[:, :q_dev, :].reshape(nblk * q_dev, feat)
    stats = join3(gathered[:, q_dev:, :].reshape(nblk, stat_rows * feat), 2 * width)
    stats = jnp.sum(stats, axis=0)

    col_sum, col_sq = stats[:width], stats[width:]
    total = library.shape[0] * nblk
    mean = col_sum / total
    spread = col_sq / total - mean * mean
    zvals = ((values - mean) * lax.rsqrt(spread + EPS)).astype(jnp.bfloat16)
    lib_sq = jnp.sum(jnp.square(library.astype(jnp.float32)), axis=1)

    numer, denom = weighted_sums(everyone, library, lib_sq, zvals)
    den_rows = -(-q_dev // width)
    den_rows += -(q_dev + den_rows) % 8
    den = jnp.pad(denom.reshape(nblk, q_dev), ((0, 0), (0, den_rows * width - q_dev)))
    den = den.reshape(nblk, den_rows, width)
    sums = jnp.concatenate([numer.reshape(nblk, q_dev, width), den], axis=1)
    sums = sums.reshape(nblk * (q_dev + den_rows), width)
    mine = lax.psum_scatter(sums, "blk", scatter_dimension=0, tiled=True)
    own_num = mine[:q_dev]
    own_den = mine[q_dev:].reshape(den_rows * width)[:q_dev]
    return own_num / own_den[:, None]


def solution(mesh):
    return jax.shard_map(
        shards,
        mesh=mesh,
        in_specs=(P(("grp", "blk"), None), P(("grp", "blk"), None), P(("grp", "blk"), None)),
        out_specs=P(("grp", "blk"), None),
        check_vma=False,
    )
```

```python
import jax
import jax.numpy as jnp
from jax import lax
from jax.sharding import PartitionSpec as P

EPS = 1e-05
TAU = 0.05


def weighted_sums(block, library, lib_sq, zvals):
    blockf = block.astype(jnp.float32)
    q_sq = jnp.sum(blockf * blockf, axis=1)
    inner = lax.dot_general(
        block, library, (((1,), (1,)), ((), ())), preferred_element_type=jnp.float32
    )
    tanimoto = inner / (q_sq[:, None] + lib_sq[None, :] - inner)
    weight = jnp.exp((tanimoto - 1.0) / TAU)
    numer = jnp.dot(weight.astype(jnp.bfloat16), zvals, preferred_element_type=jnp.float32)
    denom = jnp.sum(weight, axis=1)
    return (numer, denom)


def swap(tree, axis, dist):
    count = lax.axis_size(axis)
    return lax.ppermute(tree, axis, [(i, i ^ dist) for i in range(count)])


def shards(queries, library, assays):
    nblk = lax.axis_size("blk")
    q_dev, feat = queries.shape
    width = assays.shape[1]
    values = assays.astype(jnp.float32)
    partial = jnp.concatenate([jnp.sum(values, axis=0), jnp.sum(values * values, axis=0)])

    dists = []
    dist = nblk // 2
    while dist >= 1:
        dists.append(dist)
        dist //= 2
    qbuf, sbuf = queries[None], partial[None]
    for dist in dists:
        q_in, s_in = swap((qbuf, sbuf), "blk", dist)
        qbuf = jnp.concatenate([qbuf, q_in], axis=0)
        sbuf = jnp.concatenate([sbuf, s_in], axis=0)

    stats = jnp.sum(sbuf, axis=0)
    col_sum, col_sq = stats[:width], stats[width:]
    total = library.shape[0] * nblk
    mean = col_sum / total
    spread = col_sq / total - mean * mean
    zvals = ((values - mean) * lax.rsqrt(spread + EPS)).astype(jnp.bfloat16)
    lib_sq = jnp.sum(jnp.square(library.astype(jnp.float32)), axis=1)

    numer, denom = weighted_sums(qbuf.reshape(nblk * q_dev, feat), library, lib_sq, zvals)
    nbuf = numer.reshape(nblk, q_dev, width)
    dbuf = denom.reshape(nblk, q_dev)
    for dist in reversed(dists):
        half = nbuf.shape[0] // 2
        n_in, d_in = swap((nbuf[half:], dbuf[half:]), "blk", dist)
        nbuf = nbuf[:half] + n_in
        dbuf = dbuf[:half] + d_in
    return nbuf[0] / dbuf[0][:, None]


def solution(mesh):
    return jax.shard_map(
        shards,
        mesh=mesh,
        in_specs=(P(("grp", "blk"), None), P(("grp", "blk"), None), P(("grp", "blk"), None)),
        out_specs=P(("grp", "blk"), None),
        check_vma=False,
    )
```

```python
import jax
import jax.numpy as jnp
from jax import lax
from jax.sharding import PartitionSpec as P

EPS = 1e-05
TAU = 0.05


def split3(x):
    hi = lax.reduce_precision(x, exponent_bits=8, mantissa_bits=7)
    rest = x - hi
    mid = lax.reduce_precision(rest, exponent_bits=8, mantissa_bits=7)
    lo = rest - mid
    return jnp.concatenate([hi, mid, lo], axis=-1).astype(jnp.bfloat16)


def join3(parts, n):
    parts = parts.astype(jnp.float32)
    return (parts[..., :n] + parts[..., n:2 * n]) + parts[..., 2 * n:3 * n]


def weighted_sums(block, library, lib_sq, zvals):
    blockf = block.astype(jnp.float32)
    q_sq = jnp.sum(blockf * blockf, axis=1)
    inner = lax.dot_general(
        block, library, (((1,), (1,)), ((), ())), preferred_element_type=jnp.float32
    )
    tanimoto = inner / (q_sq[:, None] + lib_sq[None, :] - inner)
    weight = jnp.exp((tanimoto - 1.0) / TAU)
    numer = jnp.dot(weight.astype(jnp.bfloat16), zvals, preferred_element_type=jnp.float32)
    denom = jnp.sum(weight, axis=1)
    return (numer, denom)


def shards(queries, library, assays):
    nblk = lax.axis_size("blk")
    q_dev, feat = queries.shape
    width = assays.shape[1]
    values = assays.astype(jnp.float32)
    partial = jnp.concatenate([jnp.sum(values, axis=0), jnp.sum(values * values, axis=0)])

    coded = split3(partial)
    lanes = -(-coded.shape[0] // q_dev)
    lanes += -lanes % 128
    coded = jnp.pad(coded, (0, q_dev * lanes - coded.shape[0])).reshape(q_dev, lanes)
    packet = jnp.concatenate([queries, coded], axis=1)
    packets = jnp.broadcast_to(packet[None], (nblk,) + packet.shape)
    got = lax.all_to_all(packets, "blk", 0, 0, tiled=True)
    everyone = got[:, :, :feat].reshape(nblk * q_dev, feat)
    stats = join3(got[:, :, feat:].reshape(nblk, q_dev * lanes), 2 * width)
    stats = jnp.sum(stats, axis=0)

    col_sum, col_sq = stats[:width], stats[width:]
    total = library.shape[0] * nblk
    mean = col_sum / total
    spread = col_sq / total - mean * mean
    zvals = ((values - mean) * lax.rsqrt(spread + EPS)).astype(jnp.bfloat16)
    lib_sq = jnp.sum(jnp.square(library.astype(jnp.float32)), axis=1)

    numer, denom = weighted_sums(everyone, library, lib_sq, zvals)
    den_rows = -(-q_dev // width)
    den_rows += -(q_dev + den_rows) % 8
    den = jnp.pad(denom.reshape(nblk, q_dev), ((0, 0), (0, den_rows * width - q_dev)))
    den = den.reshape(nblk, den_rows, width)
    sums = jnp.concatenate([numer.reshape(nblk, q_dev, width), den], axis=1)
    mine = jnp.sum(lax.all_to_all(sums, "blk", 0, 0, tiled=True), axis=0)
    own_num = mine[:q_dev]
    own_den = mine[q_dev:].reshape(den_rows * width)[:q_dev]
    return own_num / own_den[:, None]


def solution(mesh):
    return jax.shard_map(
        shards,
        mesh=mesh,
        in_specs=(P(("grp", "blk"), None), P(("grp", "blk"), None), P(("grp", "blk"), None)),
        out_specs=P(("grp", "blk"), None),
        check_vma=False,
    )
```

```python
import jax
import jax.numpy as jnp
from jax import lax
from jax.sharding import PartitionSpec as P

EPS = 1e-05
TAU = 0.05


def split3(x):
    hi = lax.reduce_precision(x, exponent_bits=8, mantissa_bits=7)
    rest = x - hi
    mid = lax.reduce_precision(rest, exponent_bits=8, mantissa_bits=7)
    lo = rest - mid
    return jnp.concatenate([hi, mid, lo], axis=-1).astype(jnp.bfloat16)


def join3(parts, n):
    parts = parts.astype(jnp.float32)
    return (parts[..., :n] + parts[..., n:2 * n]) + parts[..., 2 * n:3 * n]


def weighted_sums(block, library, lib_sq, zvals):
    blockf = block.astype(jnp.float32)
    q_sq = jnp.sum(blockf * blockf, axis=1)
    inner = lax.dot_general(
        block, library, (((1,), (1,)), ((), ())), preferred_element_type=jnp.float32
    )
    tanimoto = inner / (q_sq[:, None] + lib_sq[None, :] - inner)
    weight = jnp.exp((tanimoto - 1.0) / TAU)
    numer = jnp.dot(weight.astype(jnp.bfloat16), zvals, preferred_element_type=jnp.float32)
    denom = jnp.sum(weight, axis=1)
    return (numer, denom)


def swap(x, axis, mask):
    count = lax.axis_size(axis)
    return lax.ppermute(x, axis, [(i, i ^ mask) for i in range(count)])


def digit_groups(count):
    bits = []
    while (1 << len(bits)) < count:
        bits.append(1 << len(bits))
    assert (1 << len(bits)) == count
    return [bits[k:k + 2] for k in range(0, len(bits), 2)]


def offsets(group):
    masks = [0]
    for bit in group:
        masks = masks + [m | bit for m in masks]
    return masks


def gather_rounds(packet, axis, groups):
    buf = packet
    for group in reversed(groups):
        parts = [buf] + [swap(buf, axis, m) for m in offsets(group)[1:]]
        buf = jnp.stack(parts, axis=0)
    return buf


def scatter_rounds(buf, axis, groups):
    for group in groups:
        masks = offsets(group)
        total = buf[0]
        for k in range(1, len(masks)):
            total = total + swap(buf[k], axis, masks[k])
        buf = total
    return buf


def shards(queries, library, assays):
    nblk = lax.axis_size("blk")
    groups = digit_groups(nblk)
    q_dev, feat = queries.shape
    width = assays.shape[1]
    values = assays.astype(jnp.float32)
    partial = jnp.concatenate([jnp.sum(values, axis=0), jnp.sum(values * values, axis=0)])

    coded = split3(partial)
    lanes = -(-coded.shape[0] // q_dev)
    lanes += -lanes % 128
    coded = jnp.pad(coded, (0, q_dev * lanes - coded.shape[0])).reshape(q_dev, lanes)
    packet = jnp.concatenate([queries, coded], axis=1)
    got = gather_rounds(packet, "blk", groups).reshape(nblk, q_dev, feat + lanes)
    everyone = got[:, :, :feat].reshape(nblk * q_dev, feat)
    stats = join3(got[:, :, feat:].reshape(nblk, q_dev * lanes), 2 * width)
    stats = jnp.sum(stats, axis=0)

    col_sum, col_sq = stats[:width], stats[width:]
    total = library.shape[0] * nblk
    mean = col_sum / total
    spread = col_sq / total - mean * mean
    zvals = ((values - mean) * lax.rsqrt(spread + EPS)).astype(jnp.bfloat16)
    lib_sq = jnp.sum(jnp.square(library.astype(jnp.float32)), axis=1)

    numer, denom = weighted_sums(everyone, library, lib_sq, zvals)
    den_rows = -(-q_dev // width)
    den_rows += -(q_dev + den_rows) % 8
    den = jnp.pad(denom.reshape(nblk, q_dev), ((0, 0), (0, den_rows * width - q_dev)))
    den = den.reshape(nblk, den_rows, width)
    sums = jnp.concatenate([numer.reshape(nblk, q_dev, width), den], axis=1)
    sums = sums.reshape(tuple(len(offsets(g)) for g in groups) + sums.shape[1:])
    mine = scatter_rounds(sums, "blk", groups)
    own_num = mine[:q_dev]
    own_den = mine[q_dev:].reshape(den_rows * width)[:q_dev]
    return own_num / own_den[:, None]


def solution(mesh):
    return jax.shard_map(
        shards,
        mesh=mesh,
        in_specs=(P(("grp", "blk"), None), P(("grp", "blk"), None), P(("grp", "blk"), None)),
        out_specs=P(("grp", "blk"), None),
        check_vma=False,
    )
```

```python
import jax
import jax.numpy as jnp
from jax import lax
from jax.sharding import PartitionSpec as P

EPS = 1e-05
TAU = 0.05


def split3(x):
    hi = lax.reduce_precision(x, exponent_bits=8, mantissa_bits=7)
    rest = x - hi
    mid = lax.reduce_precision(rest, exponent_bits=8, mantissa_bits=7)
    lo = rest - mid
    return jnp.concatenate([hi, mid, lo], axis=-1).astype(jnp.bfloat16)


def join3(parts, n):
    parts = parts.astype(jnp.float32)
    return (parts[..., :n] + parts[..., n:2 * n]) + parts[..., 2 * n:3 * n]


def weighted_sums(block, library, lib_sq, zvals):
    blockf = block.astype(jnp.float32)
    q_sq = jnp.sum(blockf * blockf, axis=1)
    inner = lax.dot_general(
        block, library, (((1,), (1,)), ((), ())), preferred_element_type=jnp.float32
    )
    tanimoto = inner / (q_sq[:, None] + lib_sq[None, :] - inner)
    weight = jnp.exp((tanimoto - 1.0) / TAU)
    numer = jnp.dot(weight.astype(jnp.bfloat16), zvals, preferred_element_type=jnp.float32)
    denom = jnp.sum(weight, axis=1)
    return (numer, denom)


def swap(x, axis, mask):
    count = lax.axis_size(axis)
    return lax.ppermute(x, axis, [(i, i ^ mask) for i in range(count)])


def digit_groups(count):
    bits = []
    while (1 << len(bits)) < count:
        bits.append(1 << len(bits))
    assert (1 << len(bits)) == count
    groups = [bits[:1], bits[1:2]]
    rest = bits[2:]
    while rest:
        groups.insert(2, rest[-2:])
        rest = rest[:-2]
    return [g for g in groups if g]


def offsets(group):
    masks = [0]
    for bit in group:
        masks = masks + [m | bit for m in masks]
    return masks


def gather_rounds(packet, axis, groups):
    buf = packet
    for group in reversed(groups):
        parts = [buf] + [swap(buf, axis, m) for m in offsets(group)[1:]]
        buf = jnp.stack(parts, axis=0)
    return buf


def scatter_rounds(buf, axis, groups):
    for group in groups:
        masks = offsets(group)
        total = buf[0]
        for k in range(1, len(masks)):
            total = total + swap(buf[k], axis, masks[k])
        buf = total
    return buf


def shards(queries, library, assays):
    nblk = lax.axis_size("blk")
    groups = digit_groups(nblk)
    q_dev, feat = queries.shape
    width = assays.shape[1]
    values = assays.astype(jnp.float32)
    partial = jnp.concatenate([jnp.sum(values, axis=0), jnp.sum(values * values, axis=0)])

    coded = split3(partial)
    lanes = -(-coded.shape[0] // q_dev)
    lanes += -lanes % 128
    coded = jnp.pad(coded, (0, q_dev * lanes - coded.shape[0])).reshape(q_dev, lanes)
    packet = jnp.concatenate([queries, coded], axis=1)
    got = gather_rounds(packet, "blk", groups).reshape(nblk, q_dev, feat + lanes)
    everyone = got[:, :, :feat].reshape(nblk * q_dev, feat)
    stats = join3(got[:, :, feat:].reshape(nblk, q_dev * lanes), 2 * width)
    stats = jnp.sum(stats, axis=0)

    col_sum, col_sq = stats[:width], stats[width:]
    total = library.shape[0] * nblk
    mean = col_sum / total
    spread = col_sq / total - mean * mean
    zvals = ((values - mean) * lax.rsqrt(spread + EPS)).astype(jnp.bfloat16)
    lib_sq = jnp.sum(jnp.square(library.astype(jnp.float32)), axis=1)

    numer, denom = weighted_sums(everyone, library, lib_sq, zvals)
    den_rows = -(-q_dev // width)
    den_rows += -(q_dev + den_rows) % 8
    den = jnp.pad(denom.reshape(nblk, q_dev), ((0, 0), (0, den_rows * width - q_dev)))
    den = den.reshape(nblk, den_rows, width)
    sums = jnp.concatenate([numer.reshape(nblk, q_dev, width), den], axis=1)
    sums = sums.reshape(tuple(len(offsets(g)) for g in groups) + sums.shape[1:])
    mine = scatter_rounds(sums, "blk", groups)
    own_num = mine[:q_dev]
    own_den = mine[q_dev:].reshape(den_rows * width)[:q_dev]
    return own_num / own_den[:, None]


def solution(mesh):
    return jax.shard_map(
        shards,
        mesh=mesh,
        in_specs=(P(("grp", "blk"), None), P(("grp", "blk"), None), P(("grp", "blk"), None)),
        out_specs=P(("grp", "blk"), None),
        check_vma=False,
    )
```

```python
import jax
import jax.numpy as jnp
from jax import lax
from jax.sharding import PartitionSpec as P

EPS = 1e-05
TAU = 0.05


def split3(x):
    hi = lax.reduce_precision(x, exponent_bits=8, mantissa_bits=7)
    rest = x - hi
    mid = lax.reduce_precision(rest, exponent_bits=8, mantissa_bits=7)
    lo = rest - mid
    return jnp.concatenate([hi, mid, lo], axis=-1).astype(jnp.bfloat16)


def join3(parts, n):
    parts = parts.astype(jnp.float32)
    return (parts[..., :n] + parts[..., n:2 * n]) + parts[..., 2 * n:3 * n]


def weighted_sums(block, library, lib_sq, zvals):
    blockf = block.astype(jnp.float32)
    q_sq = jnp.sum(blockf * blockf, axis=1)
    inner = lax.dot_general(
        block, library, (((1,), (1,)), ((), ())), preferred_element_type=jnp.float32
    )
    tanimoto = inner / (q_sq[:, None] + lib_sq[None, :] - inner)
    weight = jnp.exp((tanimoto - 1.0) / TAU)
    numer = jnp.dot(weight.astype(jnp.bfloat16), zvals, preferred_element_type=jnp.float32)
    denom = jnp.sum(weight, axis=1)
    return (numer, denom)


def swap(x, axis, mask):
    count = lax.axis_size(axis)
    return lax.ppermute(x, axis, [(i, i ^ mask) for i in range(count)])


def digit_groups(count):
    bits = []
    while (1 << len(bits)) < count:
        bits.append(1 << len(bits))
    assert (1 << len(bits)) == count
    return [[bit] for bit in bits]


def offsets(group):
    masks = [0]
    for bit in group:
        masks = masks + [m | bit for m in masks]
    return masks


def gather_rounds(packet, axis, groups):
    buf = packet
    for group in reversed(groups):
        parts = [buf] + [swap(buf, axis, m) for m in offsets(group)[1:]]
        buf = jnp.stack(parts, axis=0)
    return buf


def scatter_rounds(buf, axis, groups):
    for group in groups:
        masks = offsets(group)
        total = buf[0]
        for k in range(1, len(masks)):
            total = total + swap(buf[k], axis, masks[k])
        buf = total
    return buf


def shards(queries, library, assays):
    nblk = lax.axis_size("blk")
    groups = digit_groups(nblk)
    q_dev, feat = queries.shape
    width = assays.shape[1]
    values = assays.astype(jnp.float32)
    partial = jnp.concatenate([jnp.sum(values, axis=0), jnp.sum(values * values, axis=0)])

    coded = split3(partial)
    lanes = -(-coded.shape[0] // q_dev)
    lanes += -lanes % 128
    coded = jnp.pad(coded, (0, q_dev * lanes - coded.shape[0])).reshape(q_dev, lanes)
    packet = jnp.concatenate([queries, coded], axis=1)
    got = gather_rounds(packet, "blk", groups).reshape(nblk, q_dev, feat + lanes)
    everyone = got[:, :, :feat].reshape(nblk * q_dev, feat)
    stats = join3(got[:, :, feat:].reshape(nblk, q_dev * lanes), 2 * width)
    stats = jnp.sum(stats, axis=0)

    col_sum, col_sq = stats[:width], stats[width:]
    total = library.shape[0] * nblk
    mean = col_sum / total
    spread = col_sq / total - mean * mean
    zvals = ((values - mean) * lax.rsqrt(spread + EPS)).astype(jnp.bfloat16)
    lib_sq = jnp.sum(jnp.square(library.astype(jnp.float32)), axis=1)

    numer, denom = weighted_sums(everyone, library, lib_sq, zvals)
    den_rows = -(-q_dev // width)
    den_rows += -(q_dev + den_rows) % 8
    den = jnp.pad(denom.reshape(nblk, q_dev), ((0, 0), (0, den_rows * width - q_dev)))
    den = den.reshape(nblk, den_rows, width)
    sums = jnp.concatenate([numer.reshape(nblk, q_dev, width), den], axis=1)
    sums = sums.reshape(tuple(len(offsets(g)) for g in groups) + sums.shape[1:])
    mine = scatter_rounds(sums, "blk", groups)
    own_num = mine[:q_dev]
    own_den = mine[q_dev:].reshape(den_rows * width)[:q_dev]
    return own_num / own_den[:, None]


def solution(mesh):
    return jax.shard_map(
        shards,
        mesh=mesh,
        in_specs=(P(("grp", "blk"), None), P(("grp", "blk"), None), P(("grp", "blk"), None)),
        out_specs=P(("grp", "blk"), None),
        check_vma=False,
    )
```

```python
import jax
import jax.numpy as jnp
from jax import lax
from jax.sharding import PartitionSpec as P

EPS = 1e-05
TAU = 0.05


def split3(x):
    hi = lax.reduce_precision(x, exponent_bits=8, mantissa_bits=7)
    rest = x - hi
    mid = lax.reduce_precision(rest, exponent_bits=8, mantissa_bits=7)
    lo = rest - mid
    return jnp.concatenate([hi, mid, lo], axis=-1).astype(jnp.bfloat16)


def join3(parts, n):
    parts = parts.astype(jnp.float32)
    return (parts[..., :n] + parts[..., n:2 * n]) + parts[..., 2 * n:3 * n]


def piece_weights(piece, lib_ext, lib_sq, feat):
    rows = piece.reshape(-1, piece.shape[-1])
    blockf = rows[:, :feat].astype(jnp.float32)
    q_sq = jnp.sum(blockf * blockf, axis=1)
    inner = lax.dot_general(
        rows, lib_ext, (((1,), (1,)), ((), ())), preferred_element_type=jnp.float32
    )
    tanimoto = inner / (q_sq[:, None] + lib_sq[None, :] - inner)
    weight = jnp.exp((tanimoto - 1.0) / TAU)
    return weight.astype(jnp.bfloat16), jnp.sum(weight, axis=1)


def swap(x, axis, mask):
    count = lax.axis_size(axis)
    return lax.ppermute(x, axis, [(i, i ^ mask) for i in range(count)])


def digit_groups(count):
    bits = []
    while (1 << len(bits)) < count:
        bits.append(1 << len(bits))
    assert (1 << len(bits)) == count
    groups = [bits[:1], bits[1:2]]
    rest = bits[2:]
    while rest:
        groups.insert(2, rest[-2:])
        rest = rest[:-2]
    return [g for g in groups if g]


def offsets(group):
    masks = [0]
    for bit in group:
        masks = masks + [m | bit for m in masks]
    return masks


def gather_rounds(packet, axis, groups, work):
    pieces = [packet[None]]
    results = [work(pieces[0])]
    for group in reversed(groups):
        buf = jnp.concatenate(pieces, axis=0) if len(pieces) > 1 else pieces[0]
        for m in offsets(group)[1:]:
            got = swap(buf, axis, m)
            pieces.append(got)
            results.append(work(got))
    return jnp.concatenate(pieces, axis=0), results


def scatter_rounds(buf, axis, groups):
    for group in groups:
        masks = offsets(group)
        total = buf[0]
        for k in range(1, len(masks)):
            total = total + swap(buf[k], axis, masks[k])
        buf = total
    return buf


def shards(queries, library, assays):
    nblk = lax.axis_size("blk")
    groups = digit_groups(nblk)
    q_dev, feat = queries.shape
    width = assays.shape[1]
    values = assays.astype(jnp.float32)
    partial = jnp.concatenate([jnp.sum(values, axis=0), jnp.sum(values * values, axis=0)])

    coded = split3(partial)
    lanes = -(-coded.shape[0] // q_dev)
    lanes += -lanes % 128
    coded = jnp.pad(coded, (0, q_dev * lanes - coded.shape[0])).reshape(q_dev, lanes)
    packet = jnp.concatenate([queries, coded], axis=1)
    lib_ext = jnp.pad(library, ((0, 0), (0, lanes)))
    lib_sq = jnp.sum(jnp.square(library.astype(jnp.float32)), axis=1)
    got, parts = gather_rounds(
        packet, "blk", groups, lambda piece: piece_weights(piece, lib_ext, lib_sq, feat)
    )
    stats = join3(got[:, :, feat:].reshape(nblk, q_dev * lanes), 2 * width)
    stats = jnp.sum(stats, axis=0)

    col_sum, col_sq = stats[:width], stats[width:]
    total = library.shape[0] * nblk
    mean = col_sum / total
    spread = col_sq / total - mean * mean
    zvals = ((values - mean) * lax.rsqrt(spread + EPS)).astype(jnp.bfloat16)

    weight_b = jnp.concatenate([p[0] for p in parts], axis=0)
    denom = jnp.concatenate([p[1] for p in parts], axis=0)
    numer = jnp.dot(weight_b, zvals, preferred_element_type=jnp.float32)
    den_rows = -(-q_dev // width)
    den_rows += -(q_dev + den_rows) % 8
    den = jnp.pad(denom.reshape(nblk, q_dev), ((0, 0), (0, den_rows * width - q_dev)))
    den = den.reshape(nblk, den_rows, width)
    sums = jnp.concatenate([numer.reshape(nblk, q_dev, width), den], axis=1)
    sums = sums.reshape(tuple(len(offsets(g)) for g in groups) + sums.shape[1:])
    mine = scatter_rounds(sums, "blk", groups)
    own_num = mine[:q_dev]
    own_den = mine[q_dev:].reshape(den_rows * width)[:q_dev]
    return own_num / own_den[:, None]


def solution(mesh):
    return jax.shard_map(
        shards,
        mesh=mesh,
        in_specs=(P(("grp", "blk"), None), P(("grp", "blk"), None), P(("grp", "blk"), None)),
        out_specs=P(("grp", "blk"), None),
        check_vma=False,
    )
```

```python
import jax
import jax.numpy as jnp
from jax import lax
from jax.sharding import PartitionSpec as P

EPS = 1e-05
TAU = 0.05


def split3(x):
    hi = lax.reduce_precision(x, exponent_bits=8, mantissa_bits=7)
    rest = x - hi
    mid = lax.reduce_precision(rest, exponent_bits=8, mantissa_bits=7)
    lo = rest - mid
    return jnp.concatenate([hi, mid, lo], axis=-1).astype(jnp.bfloat16)


def join3(parts, n):
    parts = parts.astype(jnp.float32)
    return (parts[..., :n] + parts[..., n:2 * n]) + parts[..., 2 * n:3 * n]


def piece_weights(piece, lib_ext, lib_sq, feat):
    rows = piece.reshape(-1, piece.shape[-1])
    blockf = rows[:, :feat].astype(jnp.float32)
    q_sq = jnp.sum(blockf * blockf, axis=1)
    inner = lax.dot_general(
        rows, lib_ext, (((1,), (1,)), ((), ())), preferred_element_type=jnp.float32
    )
    tanimoto = inner / (q_sq[:, None] + lib_sq[None, :] - inner)
    weight = jnp.exp((tanimoto - 1.0) / TAU)
    return weight.astype(jnp.bfloat16), jnp.sum(weight, axis=1)


def swap(x, axis, mask):
    count = lax.axis_size(axis)
    return lax.ppermute(x, axis, [(i, i ^ mask) for i in range(count)])


def digit_groups(count):
    bits = []
    while (1 << len(bits)) < count:
        bits.append(1 << len(bits))
    assert (1 << len(bits)) == count
    groups = [bits[:1], bits[1:2]]
    rest = bits[2:]
    while rest:
        groups.insert(2, rest[-2:])
        rest = rest[:-2]
    return [g for g in groups if g]


def offsets(group):
    masks = [0]
    for bit in group:
        masks = masks + [m | bit for m in masks]
    return masks


def gather_rounds(packet, axis, groups, work):
    pieces = [packet[None]]
    results = [work(pieces[0])]
    for group in reversed(groups):
        buf = jnp.concatenate(pieces, axis=0) if len(pieces) > 1 else pieces[0]
        for m in offsets(group)[1:]:
            got = swap(buf, axis, m)
            pieces.append(got)
            results.append(work(got))
    return jnp.concatenate(pieces, axis=0), results


def scatter_rounds(buf, axis, groups, fan=4):
    rounds = []
    for group in groups:
        if rounds and sum(len(g) for g in rounds[-1]) + len(group) <= fan:
            rounds[-1].append(group)
        else:
            rounds.append([group])
    for take in rounds:
        masks = [0]
        for group in take:
            masks = [a | b for a in masks for b in offsets(group)]
        flat = buf.reshape((len(masks),) + buf.shape[len(take):])
        total = flat[0]
        for k in range(1, len(masks)):
            total = total + swap(flat[k], axis, masks[k])
        buf = total
    return buf


def shards(queries, library, assays):
    nblk = lax.axis_size("blk")
    groups = digit_groups(nblk)
    q_dev, feat = queries.shape
    width = assays.shape[1]
    values = assays.astype(jnp.float32)
    partial = jnp.concatenate([jnp.sum(values, axis=0), jnp.sum(values * values, axis=0)])

    coded = split3(partial)
    lanes = -(-coded.shape[0] // q_dev)
    lanes += -lanes % 128
    coded = jnp.pad(coded, (0, q_dev * lanes - coded.shape[0])).reshape(q_dev, lanes)
    packet = jnp.concatenate([queries, coded], axis=1)
    lib_ext = jnp.pad(library, ((0, 0), (0, lanes)))
    lib_sq = jnp.sum(jnp.square(library.astype(jnp.float32)), axis=1)
    got, parts = gather_rounds(
        packet, "blk", groups, lambda piece: piece_weights(piece, lib_ext, lib_sq, feat)
    )
    stats = join3(got[:, :, feat:].reshape(nblk, q_dev * lanes), 2 * width)
    stats = jnp.sum(stats, axis=0)

    col_sum, col_sq = stats[:width], stats[width:]
    total = library.shape[0] * nblk
    mean = col_sum / total
    spread = col_sq / total - mean * mean
    zvals = ((values - mean) * lax.rsqrt(spread + EPS)).astype(jnp.bfloat16)

    weight_b = jnp.concatenate([p[0] for p in parts], axis=0)
    denom = jnp.concatenate([p[1] for p in parts], axis=0)
    numer = jnp.dot(weight_b, zvals, preferred_element_type=jnp.float32)
    den_rows = -(-q_dev // width)
    den_rows += -(q_dev + den_rows) % 8
    den = jnp.pad(denom.reshape(nblk, q_dev), ((0, 0), (0, den_rows * width - q_dev)))
    den = den.reshape(nblk, den_rows, width)
    sums = jnp.concatenate([numer.reshape(nblk, q_dev, width), den], axis=1)
    sums = sums.reshape(tuple(len(offsets(g)) for g in groups) + sums.shape[1:])
    mine = scatter_rounds(sums, "blk", groups)
    own_num = mine[:q_dev]
    own_den = mine[q_dev:].reshape(den_rows * width)[:q_dev]
    return own_num / own_den[:, None]


def solution(mesh):
    return jax.shard_map(
        shards,
        mesh=mesh,
        in_specs=(P(("grp", "blk"), None), P(("grp", "blk"), None), P(("grp", "blk"), None)),
        out_specs=P(("grp", "blk"), None),
        check_vma=False,
    )
```

```python
import jax
import jax.numpy as jnp
from jax import lax
from jax.sharding import PartitionSpec as P

EPS = 1e-05
TAU = 0.05


def split3(x):
    hi = lax.reduce_precision(x, exponent_bits=8, mantissa_bits=7)
    rest = x - hi
    mid = lax.reduce_precision(rest, exponent_bits=8, mantissa_bits=7)
    lo = rest - mid
    return jnp.concatenate([hi, mid, lo], axis=-1).astype(jnp.bfloat16)


def join3(parts, n):
    parts = parts.astype(jnp.float32)
    return (parts[..., :n] + parts[..., n:2 * n]) + parts[..., 2 * n:3 * n]


def piece_weights(piece, lib_ext, lib_sq, feat):
    rows = piece.reshape(-1, piece.shape[-1])
    blockf = rows[:, :feat].astype(jnp.float32)
    q_sq = jnp.sum(blockf * blockf, axis=1)
    inner = lax.dot_general(
        rows, lib_ext, (((1,), (1,)), ((), ())), preferred_element_type=jnp.float32
    )
    tanimoto = inner / (q_sq[:, None] + lib_sq[None, :] - inner)
    weight = jnp.exp((tanimoto - 1.0) / TAU)
    return weight.astype(jnp.bfloat16), jnp.sum(weight, axis=1)


def swap(x, axis, mask):
    count = lax.axis_size(axis)
    return lax.ppermute(x, axis, [(i, i ^ mask) for i in range(count)])


def digit_groups(count):
    bits = []
    while (1 << len(bits)) < count:
        bits.append(1 << len(bits))
    assert (1 << len(bits)) == count
    groups = [bits[:1], bits[1:2]]
    rest = bits[2:]
    while rest:
        groups.insert(2, rest[-2:])
        rest = rest[:-2]
    return [g for g in groups if g]


def offsets(group):
    masks = [0]
    for bit in group:
        masks = masks + [m | bit for m in masks]
    return masks


def gather_rounds(packet, axis, groups, work):
    pieces = [packet[None]]
    results = [work(pieces[0])]
    for group in reversed(groups):
        buf = jnp.concatenate(pieces, axis=0) if len(pieces) > 1 else pieces[0]
        for m in offsets(group)[1:]:
            got = swap(buf, axis, m)
            pieces.append(got)
            results.append(work(got))
    return jnp.concatenate(pieces, axis=0), results


def scatter_rounds(buf, axis, groups):
    for group in groups:
        masks = offsets(group)
        total = buf[0]
        for k in range(1, len(masks)):
            total = total + swap(buf[k], axis, masks[k])
        buf = total
    return buf


def shards(queries, library, assays):
    nblk = lax.axis_size("blk")
    groups = digit_groups(nblk)
    q_dev, feat = queries.shape
    width = assays.shape[1]
    values = assays.astype(jnp.float32)
    grouped = values.reshape(-1, 8, width)
    firsts = lax.optimization_barrier(
        (jnp.sum(grouped, axis=0), jnp.sum(grouped * grouped, axis=0))
    )
    partial = jnp.concatenate([jnp.sum(firsts[0], axis=0), jnp.sum(firsts[1], axis=0)])

    coded = split3(partial)
    lanes = -(-coded.shape[0] // q_dev)
    lanes += -lanes % 128
    coded = jnp.pad(coded, (0, q_dev * lanes - coded.shape[0])).reshape(q_dev, lanes)
    packet = jnp.concatenate([queries, coded], axis=1)
    lib_ext = jnp.pad(library, ((0, 0), (0, lanes)))
    lib_sq = jnp.sum(jnp.square(library.astype(jnp.float32)), axis=1)
    got, parts = gather_rounds(
        packet, "blk", groups, lambda piece: piece_weights(piece, lib_ext, lib_sq, feat)
    )
    stats = join3(got[:, :, feat:].reshape(nblk, q_dev * lanes), 2 * width)
    stats = jnp.sum(stats, axis=0)

    col_sum, col_sq = stats[:width], stats[width:]
    total = library.shape[0] * nblk
    mean = col_sum / total
    spread = col_sq / total - mean * mean
    zvals = ((values - mean) * lax.rsqrt(spread + EPS)).astype(jnp.bfloat16)

    weight_b = jnp.concatenate([p[0] for p in parts], axis=0)
    denom = jnp.concatenate([p[1] for p in parts], axis=0)
    numer = jnp.dot(weight_b, zvals, preferred_element_type=jnp.float32)
    den_rows = -(-q_dev // width)
    den_rows += -(q_dev + den_rows) % 8
    den = jnp.pad(denom.reshape(nblk, q_dev), ((0, 0), (0, den_rows * width - q_dev)))
    den = den.reshape(nblk, den_rows, width)
    sums = jnp.concatenate([numer.reshape(nblk, q_dev, width), den], axis=1)
    sums = sums.reshape(tuple(len(offsets(g)) for g in groups) + sums.shape[1:])
    mine = scatter_rounds(sums, "blk", groups)
    own_num = mine[:q_dev]
    own_den = mine[q_dev:].reshape(den_rows * width)[:q_dev]
    return own_num / own_den[:, None]


def solution(mesh):
    return jax.shard_map(
        shards,
        mesh=mesh,
        in_specs=(P(("grp", "blk"), None), P(("grp", "blk"), None), P(("grp", "blk"), None)),
        out_specs=P(("grp", "blk"), None),
        check_vma=False,
    )
```

```python
import jax
import jax.numpy as jnp
from jax import lax
from jax.sharding import PartitionSpec as P

EPS = 1e-05
TAU = 0.05


def split3(x):
    hi = lax.reduce_precision(x, exponent_bits=8, mantissa_bits=7)
    rest = x - hi
    mid = lax.reduce_precision(rest, exponent_bits=8, mantissa_bits=7)
    lo = rest - mid
    return jnp.concatenate([hi, mid, lo], axis=-1).astype(jnp.bfloat16)


def join3(parts, n):
    parts = parts.astype(jnp.float32)
    return (parts[..., :n] + parts[..., n:2 * n]) + parts[..., 2 * n:3 * n]


def piece_weights(piece, lib_ext, lib_sq, feat):
    rows = piece.reshape(-1, piece.shape[-1])
    blockf = rows[:, :feat].astype(jnp.float32)
    q_sq = jnp.sum(blockf * blockf, axis=1)
    inner = lax.dot_general(
        rows, lib_ext, (((1,), (1,)), ((), ())), preferred_element_type=jnp.float32
    )
    tanimoto = inner / (q_sq[:, None] + lib_sq[None, :] - inner)
    weight = jnp.exp((tanimoto - 1.0) / TAU)
    return weight.astype(jnp.bfloat16), jnp.sum(weight, axis=1)


def swap(x, axis, mask):
    count = lax.axis_size(axis)
    return lax.ppermute(x, axis, [(i, i ^ mask) for i in range(count)])


def digit_groups(count):
    bits = []
    while (1 << len(bits)) < count:
        bits.append(1 << len(bits))
    assert (1 << len(bits)) == count
    groups = [bits[:1], bits[1:2]]
    rest = bits[2:]
    while rest:
        groups.insert(2, rest[-2:])
        rest = rest[:-2]
    return [g for g in groups if g]


def offsets(group):
    masks = [0]
    for bit in group:
        masks = masks + [m | bit for m in masks]
    return masks


def gather_rounds(packet, axis, groups, work):
    pieces = [packet[None]]
    results = [work(pieces[0])]
    for group in reversed(groups):
        buf = jnp.concatenate(pieces, axis=0) if len(pieces) > 1 else pieces[0]
        for m in offsets(group)[1:]:
            got = swap(buf, axis, m)
            pieces.append(got)
            results.append(work(got))
    return jnp.concatenate(pieces, axis=0), results


def scatter_rounds(buf, axis, groups, fan=3):
    rounds = [[groups[0]]]
    for group in groups[1:]:
        if len(rounds) > 1 and sum(len(g) for g in rounds[-1]) + len(group) <= fan:
            rounds[-1].append(group)
        else:
            rounds.append([group])
    for take in rounds:
        masks = [0]
        for group in take:
            masks = [a | b for a in masks for b in offsets(group)]
        flat = buf.reshape((len(masks),) + buf.shape[len(take):])
        total = flat[0]
        for k in range(1, len(masks)):
            total = total + swap(flat[k], axis, masks[k])
        buf = total
    return buf


def shards(queries, library, assays):
    nblk = lax.axis_size("blk")
    groups = digit_groups(nblk)
    q_dev, feat = queries.shape
    width = assays.shape[1]
    values = assays.astype(jnp.float32)
    partial = jnp.concatenate([jnp.sum(values, axis=0), jnp.sum(values * values, axis=0)])

    coded = split3(partial)
    lanes = -(-coded.shape[0] // q_dev)
    lanes += -lanes % 128
    coded = jnp.pad(coded, (0, q_dev * lanes - coded.shape[0])).reshape(q_dev, lanes)
    packet = jnp.concatenate([queries, coded], axis=1)
    lib_ext = jnp.pad(library, ((0, 0), (0, lanes)))
    lib_sq = jnp.sum(jnp.square(library.astype(jnp.float32)), axis=1)
    got, parts = gather_rounds(
        packet, "blk", groups, lambda piece: piece_weights(piece, lib_ext, lib_sq, feat)
    )
    stats = join3(got[:, :, feat:].reshape(nblk, q_dev * lanes), 2 * width)
    stats = jnp.sum(stats, axis=0)

    col_sum, col_sq = stats[:width], stats[width:]
    total = library.shape[0] * nblk
    mean = col_sum / total
    spread = col_sq / total - mean * mean
    zvals = ((values - mean) * lax.rsqrt(spread + EPS)).astype(jnp.bfloat16)

    weight_b = jnp.concatenate([p[0] for p in parts], axis=0)
    denom = jnp.concatenate([p[1] for p in parts], axis=0)
    numer = jnp.dot(weight_b, zvals, preferred_element_type=jnp.float32)
    den_rows = -(-q_dev // width)
    den_rows += -(q_dev + den_rows) % 8
    den = jnp.pad(denom.reshape(nblk, q_dev), ((0, 0), (0, den_rows * width - q_dev)))
    den = den.reshape(nblk, den_rows, width)
    sums = jnp.concatenate([numer.reshape(nblk, q_dev, width), den], axis=1)
    sums = sums.reshape(tuple(len(offsets(g)) for g in groups) + sums.shape[1:])
    mine = scatter_rounds(sums, "blk", groups)
    own_num = mine[:q_dev]
    own_den = mine[q_dev:].reshape(den_rows * width)[:q_dev]
    return own_num / own_den[:, None]


def solution(mesh):
    return jax.shard_map(
        shards,
        mesh=mesh,
        in_specs=(P(("grp", "blk"), None), P(("grp", "blk"), None), P(("grp", "blk"), None)),
        out_specs=P(("grp", "blk"), None),
        check_vma=False,
    )
```

```python
import jax
import jax.numpy as jnp
from jax import lax
from jax.sharding import PartitionSpec as P

EPS = 1e-05
TAU = 0.05


def split3(x):
    hi = lax.reduce_precision(x, exponent_bits=8, mantissa_bits=7)
    rest = x - hi
    mid = lax.reduce_precision(rest, exponent_bits=8, mantissa_bits=7)
    lo = rest - mid
    return jnp.concatenate([hi, mid, lo], axis=-1).astype(jnp.bfloat16)


def join3(parts, n):
    parts = parts.astype(jnp.float32)
    return (parts[..., :n] + parts[..., n:2 * n]) + parts[..., 2 * n:3 * n]


def piece_weights(piece, lib_ext, lib_sq, feat):
    rows = piece.reshape(-1, piece.shape[-1])
    blockf = rows[:, :feat].astype(jnp.float32)
    q_sq = jnp.sum(blockf * blockf, axis=1)
    inner = lax.dot_general(
        rows, lib_ext, (((1,), (1,)), ((), ())), preferred_element_type=jnp.float32
    )
    tanimoto = inner / (q_sq[:, None] + lib_sq[None, :] - inner)
    weight = jnp.exp((tanimoto - 1.0) / TAU)
    return weight.astype(jnp.bfloat16), jnp.sum(weight, axis=1)


def swap(x, axis, mask):
    count = lax.axis_size(axis)
    return lax.ppermute(x, axis, [(i, i ^ mask) for i in range(count)])


def digit_groups(count):
    bits = []
    while (1 << len(bits)) < count:
        bits.append(1 << len(bits))
    assert (1 << len(bits)) == count
    groups = [bits[:1], bits[1:2]]
    rest = bits[2:]
    while rest:
        groups.insert(2, rest[-2:])
        rest = rest[:-2]
    return [g for g in groups if g]


def offsets(group):
    masks = [0]
    for bit in group:
        masks = masks + [m | bit for m in masks]
    return masks


def gather_rounds(packet, axis, groups, work):
    pieces = [packet[None]]
    results = []
    fresh = [packet[None]]
    for group in reversed(groups):
        buf = jnp.concatenate(pieces, axis=0) if len(pieces) > 1 else pieces[0]
        got = [swap(buf, axis, m) for m in offsets(group)[1:]]
        pieces += got
        fresh += got
        results.append(work(jnp.concatenate(fresh, axis=0)))
        fresh = []
    return jnp.concatenate(pieces, axis=0), results


def scatter_rounds(buf, axis, groups):
    for group in groups:
        masks = offsets(group)
        total = buf[0]
        for k in range(1, len(masks)):
            total = total + swap(buf[k], axis, masks[k])
        buf = total
    return buf


def shards(queries, library, assays):
    nblk = lax.axis_size("blk")
    groups = digit_groups(nblk)
    q_dev, feat = queries.shape
    width = assays.shape[1]
    values = assays.astype(jnp.float32)
    partial = jnp.concatenate([jnp.sum(values, axis=0), jnp.sum(values * values, axis=0)])

    coded = split3(partial)
    lanes = -(-coded.shape[0] // q_dev)
    lanes += -lanes % 128
    coded = jnp.pad(coded, (0, q_dev * lanes - coded.shape[0])).reshape(q_dev, lanes)
    packet = jnp.concatenate([queries, coded], axis=1)
    lib_ext = jnp.pad(library, ((0, 0), (0, lanes)))
    lib_sq = jnp.sum(jnp.square(library.astype(jnp.float32)), axis=1)
    got, parts = gather_rounds(
        packet, "blk", groups, lambda piece: piece_weights(piece, lib_ext, lib_sq, feat)
    )
    stats = join3(got[:, :, feat:].reshape(nblk, q_dev * lanes), 2 * width)
    stats = jnp.sum(stats, axis=0)

    col_sum, col_sq = stats[:width], stats[width:]
    total = library.shape[0] * nblk
    mean = col_sum / total
    spread = col_sq / total - mean * mean
    zvals = ((values - mean) * lax.rsqrt(spread + EPS)).astype(jnp.bfloat16)

    weight_b = jnp.concatenate([p[0] for p in parts], axis=0)
    denom = jnp.concatenate([p[1] for p in parts], axis=0)
    numer = jnp.dot(weight_b, zvals, preferred_element_type=jnp.float32)
    den_rows = -(-q_dev // width)
    den_rows += -(q_dev + den_rows) % 8
    den = jnp.pad(denom.reshape(nblk, q_dev), ((0, 0), (0, den_rows * width - q_dev)))
    den = den.reshape(nblk, den_rows, width)
    sums = jnp.concatenate([numer.reshape(nblk, q_dev, width), den], axis=1)
    sums = sums.reshape(tuple(len(offsets(g)) for g in groups) + sums.shape[1:])
    mine = scatter_rounds(sums, "blk", groups)
    own_num = mine[:q_dev]
    own_den = mine[q_dev:].reshape(den_rows * width)[:q_dev]
    return own_num / own_den[:, None]


def solution(mesh):
    return jax.shard_map(
        shards,
        mesh=mesh,
        in_specs=(P(("grp", "blk"), None), P(("grp", "blk"), None), P(("grp", "blk"), None)),
        out_specs=P(("grp", "blk"), None),
        check_vma=False,
    )
```

```python
import jax
import jax.numpy as jnp
from jax import lax
from jax.sharding import PartitionSpec as P

EPS = 1e-05
TAU = 0.05


def split3(x):
    hi = lax.reduce_precision(x, exponent_bits=8, mantissa_bits=7)
    rest = x - hi
    mid = lax.reduce_precision(rest, exponent_bits=8, mantissa_bits=7)
    lo = rest - mid
    return jnp.concatenate([hi, mid, lo], axis=-1).astype(jnp.bfloat16)


def join3(parts, n):
    parts = parts.astype(jnp.float32)
    return (parts[..., :n] + parts[..., n:2 * n]) + parts[..., 2 * n:3 * n]


def piece_weights(piece, lib_ext, lib_sq, feat):
    rows = piece.reshape(-1, piece.shape[-1])
    blockf = rows[:, :feat].astype(jnp.float32)
    q_sq = jnp.sum(blockf * blockf, axis=1)
    inner = lax.dot_general(
        rows, lib_ext, (((1,), (1,)), ((), ())), preferred_element_type=jnp.float32
    )
    tanimoto = inner / (q_sq[:, None] + lib_sq[None, :] - inner)
    weight = jnp.exp((tanimoto - 1.0) / TAU)
    return weight.astype(jnp.bfloat16), jnp.sum(weight, axis=1)


def swap(x, axis, mask):
    count = lax.axis_size(axis)
    return lax.ppermute(x, axis, [(i, i ^ mask) for i in range(count)])


def digit_groups(count):
    bits = []
    while (1 << len(bits)) < count:
        bits.append(1 << len(bits))
    assert (1 << len(bits)) == count
    groups = [bits[:1], bits[1:2]]
    rest = bits[2:]
    while rest:
        groups.insert(2, rest[-2:])
        rest = rest[:-2]
    return [g for g in groups if g]


def offsets(group):
    masks = [0]
    for bit in group:
        masks = masks + [m | bit for m in masks]
    return masks


def gather_rounds(packet, axis, groups, work):
    pieces = [packet[None]]
    results = []
    fresh = [packet[None]]
    for group in reversed(groups):
        buf = jnp.concatenate(pieces, axis=0) if len(pieces) > 1 else pieces[0]
        got = [swap(buf, axis, m) for m in offsets(group)[1:]]
        if results:
            got, results[-1] = lax.optimization_barrier((got, results[-1]))
        pieces += got
        fresh += got
        results.append(work(jnp.concatenate(fresh, axis=0)))
        fresh = []
    return jnp.concatenate(pieces, axis=0), results


def scatter_rounds(buf, axis, groups):
    for group in groups:
        masks = offsets(group)
        total = buf[0]
        for k in range(1, len(masks)):
            total = total + swap(buf[k], axis, masks[k])
        buf = total
    return buf


def shards(queries, library, assays):
    nblk = lax.axis_size("blk")
    groups = digit_groups(nblk)
    q_dev, feat = queries.shape
    width = assays.shape[1]
    values = assays.astype(jnp.float32)
    partial = jnp.concatenate([jnp.sum(values, axis=0), jnp.sum(values * values, axis=0)])

    coded = split3(partial)
    lanes = -(-coded.shape[0] // q_dev)
    lanes += -lanes % 128
    coded = jnp.pad(coded, (0, q_dev * lanes - coded.shape[0])).reshape(q_dev, lanes)
    packet = jnp.concatenate([queries, coded], axis=1)
    lib_ext = jnp.pad(library, ((0, 0), (0, lanes)))
    lib_sq = jnp.sum(jnp.square(library.astype(jnp.float32)), axis=1)
    got, parts = gather_rounds(
        packet, "blk", groups, lambda piece: piece_weights(piece, lib_ext, lib_sq, feat)
    )
    stats = join3(got[:, :, feat:].reshape(nblk, q_dev * lanes), 2 * width)
    stats = jnp.sum(stats, axis=0)

    col_sum, col_sq = stats[:width], stats[width:]
    total = library.shape[0] * nblk
    mean = col_sum / total
    spread = col_sq / total - mean * mean
    zvals = ((values - mean) * lax.rsqrt(spread + EPS)).astype(jnp.bfloat16)

    weight_b = jnp.concatenate([p[0] for p in parts], axis=0)
    denom = jnp.concatenate([p[1] for p in parts], axis=0)
    numer = jnp.dot(weight_b, zvals, preferred_element_type=jnp.float32)
    den_rows = -(-q_dev // width)
    den_rows += -(q_dev + den_rows) % 8
    den = jnp.pad(denom.reshape(nblk, q_dev), ((0, 0), (0, den_rows * width - q_dev)))
    den = den.reshape(nblk, den_rows, width)
    sums = jnp.concatenate([numer.reshape(nblk, q_dev, width), den], axis=1)
    sums = sums.reshape(tuple(len(offsets(g)) for g in groups) + sums.shape[1:])
    mine = scatter_rounds(sums, "blk", groups)
    own_num = mine[:q_dev]
    own_den = mine[q_dev:].reshape(den_rows * width)[:q_dev]
    return own_num / own_den[:, None]


def solution(mesh):
    return jax.shard_map(
        shards,
        mesh=mesh,
        in_specs=(P(("grp", "blk"), None), P(("grp", "blk"), None), P(("grp", "blk"), None)),
        out_specs=P(("grp", "blk"), None),
        check_vma=False,
    )
```

```python
import jax
import jax.numpy as jnp
from jax import lax
from jax.sharding import PartitionSpec as P

EPS = 1e-05
TAU = 0.05


def split3(x):
    hi = lax.reduce_precision(x, exponent_bits=8, mantissa_bits=7)
    rest = x - hi
    mid = lax.reduce_precision(rest, exponent_bits=8, mantissa_bits=7)
    lo = rest - mid
    return jnp.concatenate([hi, mid, lo], axis=-1).astype(jnp.bfloat16)


def join3(parts, n):
    parts = parts.astype(jnp.float32)
    return (parts[..., :n] + parts[..., n:2 * n]) + parts[..., 2 * n:3 * n]


def piece_weights(pieces, libs, lib_sq, feat):
    inner, q_sq, start = None, None, 0
    for piece, lib in zip(pieces, libs):
        rows = piece.reshape(-1, piece.shape[-1])
        used = max(0, min(feat - start, rows.shape[1]))
        if used:
            part = rows[:, :used].astype(jnp.float32)
            part = jnp.sum(part * part, axis=1)
            q_sq = part if q_sq is None else q_sq + part
        part = lax.dot_general(
            rows, lib, (((1,), (1,)), ((), ())), preferred_element_type=jnp.float32
        )
        inner = part if inner is None else inner + part
        start += rows.shape[1]
    tanimoto = inner / (q_sq[:, None] + lib_sq[None, :] - inner)
    weight = jnp.exp((tanimoto - 1.0) / TAU)
    return weight.astype(jnp.bfloat16), jnp.sum(weight, axis=1)


def swap(x, axis, mask):
    count = lax.axis_size(axis)
    return lax.ppermute(x, axis, [(i, i ^ mask) for i in range(count)])


def digit_groups(count):
    bits = []
    while (1 << len(bits)) < count:
        bits.append(1 << len(bits))
    assert (1 << len(bits)) == count
    groups = [bits[:1], bits[1:2]]
    rest = bits[2:]
    while rest:
        groups.insert(2, rest[-2:])
        rest = rest[:-2]
    return [g for g in groups if g]


def offsets(group):
    masks = [0]
    for bit in group:
        masks = masks + [m | bit for m in masks]
    return masks


def gather_rounds(packets, axis, groups, work):
    rounds = list(reversed(groups))
    held = [[p[None]] for p in packets]
    brought = [[[p[None]] for p in packets]] + [[[] for _ in packets] for _ in rounds[1:]]
    results = []
    for stage in range(len(rounds) + len(packets) - 1):
        for s in range(len(packets)):
            r = stage - s
            if 0 <= r < len(rounds):
                buf = jnp.concatenate(held[s], axis=0) if len(held[s]) > 1 else held[s][0]
                if s:
                    buf, _ = lax.optimization_barrier((buf, brought[r][s - 1]))
                got = [swap(buf, axis, m) for m in offsets(rounds[r])[1:]]
                held[s] += got
                brought[r][s] += got
        r = stage - len(packets) + 1
        if r >= 0:
            results.append(work([jnp.concatenate(b, axis=0) for b in brought[r]]))
    return [jnp.concatenate(h, axis=0) for h in held], results


def scatter_rounds(buf, axis, groups):
    for group in groups:
        masks = offsets(group)
        total = buf[0]
        for k in range(1, len(masks)):
            total = total + swap(buf[k], axis, masks[k])
        buf = total
    return buf


def shards(queries, library, assays):
    nblk = lax.axis_size("blk")
    groups = digit_groups(nblk)
    q_dev, feat = queries.shape
    width = assays.shape[1]
    values = assays.astype(jnp.float32)
    partial = jnp.concatenate([jnp.sum(values, axis=0), jnp.sum(values * values, axis=0)])

    coded = split3(partial)
    lanes = -(-coded.shape[0] // q_dev)
    lanes += -lanes % 128
    coded = jnp.pad(coded, (0, q_dev * lanes - coded.shape[0])).reshape(q_dev, lanes)
    packet = jnp.concatenate([queries, coded], axis=1)
    lib_ext = jnp.pad(library, ((0, 0), (0, lanes)))
    lib_sq = jnp.sum(jnp.square(library.astype(jnp.float32)), axis=1)
    cut = (feat // 2) // 128 * 128
    packets = [packet[:, :cut], packet[:, cut:]]
    libs = [lib_ext[:, :cut], lib_ext[:, cut:]]
    helds, parts = gather_rounds(
        packets, "blk", groups, lambda pieces: piece_weights(pieces, libs, lib_sq, feat)
    )
    got = helds[-1]
    stat_lo = feat - cut
    stats = join3(got[:, :, stat_lo:].reshape(nblk, q_dev * lanes), 2 * width)
    stats = jnp.sum(stats, axis=0)

    col_sum, col_sq = stats[:width], stats[width:]
    total = library.shape[0] * nblk
    mean = col_sum / total
    spread = col_sq / total - mean * mean
    zvals = ((values - mean) * lax.rsqrt(spread + EPS)).astype(jnp.bfloat16)

    weight_b = jnp.concatenate([p[0] for p in parts], axis=0)
    denom = jnp.concatenate([p[1] for p in parts], axis=0)
    numer = jnp.dot(weight_b, zvals, preferred_element_type=jnp.float32)
    den_rows = -(-q_dev // width)
    den_rows += -(q_dev + den_rows) % 8
    den = jnp.pad(denom.reshape(nblk, q_dev), ((0, 0), (0, den_rows * width - q_dev)))
    den = den.reshape(nblk, den_rows, width)
    sums = jnp.concatenate([numer.reshape(nblk, q_dev, width), den], axis=1)
    sums = sums.reshape(tuple(len(offsets(g)) for g in groups) + sums.shape[1:])
    mine = scatter_rounds(sums, "blk", groups)
    own_num = mine[:q_dev]
    own_den = mine[q_dev:].reshape(den_rows * width)[:q_dev]
    return own_num / own_den[:, None]


def solution(mesh):
    return jax.shard_map(
        shards,
        mesh=mesh,
        in_specs=(P(("grp", "blk"), None), P(("grp", "blk"), None), P(("grp", "blk"), None)),
        out_specs=P(("grp", "blk"), None),
        check_vma=False,
    )
```

```python
import jax
import jax.numpy as jnp
from jax import lax
from jax.sharding import PartitionSpec as P

EPS = 1e-05
TAU = 0.05


def split3(x):
    hi = lax.reduce_precision(x, exponent_bits=8, mantissa_bits=7)
    rest = x - hi
    mid = lax.reduce_precision(rest, exponent_bits=8, mantissa_bits=7)
    lo = rest - mid
    return jnp.concatenate([hi, mid, lo], axis=-1).astype(jnp.bfloat16)


def join3(parts, n):
    parts = parts.astype(jnp.float32)
    return (parts[..., :n] + parts[..., n:2 * n]) + parts[..., 2 * n:3 * n]


def piece_weights(piece, lib_ext, lib_sq, feat):
    rows = piece.reshape(-1, piece.shape[-1])
    blockf = rows[:, :feat].astype(jnp.float32)
    q_sq = jnp.sum(blockf * blockf, axis=1)
    inner = lax.dot_general(
        rows, lib_ext, (((1,), (1,)), ((), ())), preferred_element_type=jnp.float32
    )
    tanimoto = inner / (q_sq[:, None] + lib_sq[None, :] - inner)
    weight = jnp.exp((tanimoto - 1.0) / TAU)
    return weight.astype(jnp.bfloat16), jnp.sum(weight, axis=1)


def swap(x, axis, mask):
    count = lax.axis_size(axis)
    return lax.ppermute(x, axis, [(i, i ^ mask) for i in range(count)])


def digit_groups(count):
    bits = []
    while (1 << len(bits)) < count:
        bits.append(1 << len(bits))
    assert (1 << len(bits)) == count
    groups = [bits[:1], bits[1:2]]
    rest = bits[2:]
    while rest:
        groups.insert(2, rest[-2:])
        rest = rest[:-2]
    return [g for g in groups if g]


def offsets(group):
    masks = [0]
    for bit in group:
        masks = masks + [m | bit for m in masks]
    return masks


def gather_rounds(packet, axis, groups, work):
    pieces = [packet[None]]
    results = []
    fresh = [packet[None]]
    for group in reversed(groups):
        buf = jnp.concatenate(pieces, axis=0) if len(pieces) > 1 else pieces[0]
        got = [swap(buf, axis, m) for m in offsets(group)[1:]]
        if results:
            got, results[-1] = lax.optimization_barrier((got, results[-1]))
        pieces += got
        fresh += got
        results.append(work(jnp.concatenate(fresh, axis=0)))
        fresh = []
    return jnp.concatenate(pieces, axis=0), results


def scatter_rounds(buf, axis, groups):
    for group in groups:
        masks = offsets(group)
        total = buf[0]
        for k in range(1, len(masks)):
            total = total + swap(buf[k], axis, masks[k])
        buf = total
    return buf


def shards(queries, library, assays):
    nblk = lax.axis_size("blk")
    groups = digit_groups(nblk)
    q_dev, feat = queries.shape
    width = assays.shape[1]
    values = assays.astype(jnp.float32)
    partial = jnp.concatenate([jnp.sum(values, axis=0), jnp.sum(values * values, axis=0)])

    coded = split3(partial)
    lanes = -(-coded.shape[0] // q_dev)
    lanes += -lanes % 128
    coded = jnp.pad(coded, (0, q_dev * lanes - coded.shape[0])).reshape(q_dev, lanes)
    packet = jnp.concatenate([queries, coded], axis=1)
    lib_ext = jnp.pad(library, ((0, 0), (0, lanes)))
    lib_sq = jnp.sum(jnp.square(library.astype(jnp.float32)), axis=1)
    got, parts = gather_rounds(
        packet, "blk", groups, lambda piece: piece_weights(piece, lib_ext, lib_sq, feat)
    )
    stats = join3(got[:, :, feat:].reshape(nblk, q_dev * lanes), 2 * width)
    stats = jnp.sum(stats, axis=0)

    col_sum, col_sq = stats[:width], stats[width:]
    total = library.shape[0] * nblk
    mean = col_sum / total
    spread = col_sq / total - mean * mean
    zvals = ((values - mean) * lax.rsqrt(spread + EPS)).astype(jnp.bfloat16)

    weight_b = jnp.concatenate([p[0] for p in parts], axis=0)
    denom = jnp.concatenate([p[1] for p in parts], axis=0)
    numer = jnp.dot(weight_b, zvals, preferred_element_type=jnp.float32)
    den = jnp.broadcast_to(denom[:, None], (denom.shape[0], 128))
    sums = jnp.concatenate([numer, den], axis=1).reshape(nblk, q_dev, width + 128)
    sums = sums.reshape(tuple(len(offsets(g)) for g in groups) + sums.shape[1:])
    mine = scatter_rounds(sums, "blk", groups)
    return mine[:, :width] / mine[:, width:width + 1]


def solution(mesh):
    return jax.shard_map(
        shards,
        mesh=mesh,
        in_specs=(P(("grp", "blk"), None), P(("grp", "blk"), None), P(("grp", "blk"), None)),
        out_specs=P(("grp", "blk"), None),
        check_vma=False,
    )
```

```python
import jax
import jax.numpy as jnp
from jax import lax
from jax.sharding import PartitionSpec as P

EPS = 1e-05
TAU = 0.05


def split3(x):
    hi = lax.reduce_precision(x, exponent_bits=8, mantissa_bits=7)
    rest = x - hi
    mid = lax.reduce_precision(rest, exponent_bits=8, mantissa_bits=7)
    lo = rest - mid
    return jnp.concatenate([hi, mid, lo], axis=-1).astype(jnp.bfloat16)


def join3(parts, n):
    parts = parts.astype(jnp.float32)
    return (parts[..., :n] + parts[..., n:2 * n]) + parts[..., 2 * n:3 * n]


def piece_weights(piece, lib_ext, lib_sq, feat):
    rows = piece.reshape(-1, piece.shape[-1])
    blockf = rows[:, :feat].astype(jnp.float32)
    q_sq = jnp.sum(blockf * blockf, axis=1)
    inner = lax.dot_general(
        rows, lib_ext, (((1,), (1,)), ((), ())), preferred_element_type=jnp.float32
    )
    tanimoto = inner / (q_sq[:, None] + lib_sq[None, :] - inner)
    weight = jnp.exp((tanimoto - 1.0) / TAU)
    return weight.astype(jnp.bfloat16), jnp.sum(weight, axis=1)


def swap(x, axis, mask):
    count = lax.axis_size(axis)
    return lax.ppermute(x, axis, [(i, i ^ mask) for i in range(count)])


def digit_groups(count):
    bits = []
    while (1 << len(bits)) < count:
        bits.append(1 << len(bits))
    assert (1 << len(bits)) == count
    groups = [bits[:1], bits[1:2]]
    rest = bits[2:]
    while rest:
        groups.insert(2, rest[-2:])
        rest = rest[:-2]
    return [g for g in groups if g]


def offsets(group):
    masks = [0]
    for bit in group:
        masks = masks + [m | bit for m in masks]
    return masks


def gather_rounds(packet, axis, groups, work):
    rounds = list(reversed(groups))
    pieces = [packet[None]]
    results = []
    fresh = [packet[None]]
    early = []
    for r, group in enumerate(rounds):
        buf = jnp.concatenate(pieces, axis=0) if len(pieces) > 1 else pieces[0]
        if r == 1:
            got = [
                [head, swap(buf[1:], axis, m)]
                for head, m in zip(early, offsets(group)[1:])
            ]
            got = [g for pair in got for g in pair]
        else:
            got = [swap(buf, axis, m) for m in offsets(group)[1:]]
        if r == 0 and len(rounds) > 1:
            early = [swap(packet[None], axis, m) for m in offsets(rounds[1])[1:]]
        if results:
            got, results[-1] = lax.optimization_barrier((got, results[-1]))
        pieces += got
        fresh += got
        results.append(work(jnp.concatenate(fresh, axis=0)))
        fresh = []
    return jnp.concatenate(pieces, axis=0), results


def scatter_rounds(buf, axis, groups):
    for group in groups:
        masks = offsets(group)
        total = buf[0]
        for k in range(1, len(masks)):
            total = total + swap(buf[k], axis, masks[k])
        buf = total
    return buf


def shards(queries, library, assays):
    nblk = lax.axis_size("blk")
    groups = digit_groups(nblk)
    q_dev, feat = queries.shape
    width = assays.shape[1]
    values = assays.astype(jnp.float32)
    partial = jnp.concatenate([jnp.sum(values, axis=0), jnp.sum(values * values, axis=0)])

    coded = split3(partial)
    lanes = -(-coded.shape[0] // q_dev)
    lanes += -lanes % 128
    coded = jnp.pad(coded, (0, q_dev * lanes - coded.shape[0])).reshape(q_dev, lanes)
    packet = jnp.concatenate([queries, coded], axis=1)
    lib_ext = jnp.pad(library, ((0, 0), (0, lanes)))
    lib_sq = jnp.sum(jnp.square(library.astype(jnp.float32)), axis=1)
    got, parts = gather_rounds(
        packet, "blk", groups, lambda piece: piece_weights(piece, lib_ext, lib_sq, feat)
    )
    stats = join3(got[:, :, feat:].reshape(nblk, q_dev * lanes), 2 * width)
    stats = jnp.sum(stats, axis=0)

    col_sum, col_sq = stats[:width], stats[width:]
    total = library.shape[0] * nblk
    mean = col_sum / total
    spread = col_sq / total - mean * mean
    zvals = ((values - mean) * lax.rsqrt(spread + EPS)).astype(jnp.bfloat16)

    weight_b = jnp.concatenate([p[0] for p in parts], axis=0)
    denom = jnp.concatenate([p[1] for p in parts], axis=0)
    numer = jnp.dot(weight_b, zvals, preferred_element_type=jnp.float32)
    den = jnp.broadcast_to(denom[:, None], (denom.shape[0], 128))
    sums = jnp.concatenate([numer, den], axis=1).reshape(nblk, q_dev, width + 128)
    sums = sums.reshape(tuple(len(offsets(g)) for g in groups) + sums.shape[1:])
    mine = scatter_rounds(sums, "blk", groups)
    return mine[:, :width] / mine[:, width:width + 1]


def solution(mesh):
    return jax.shard_map(
        shards,
        mesh=mesh,
        in_specs=(P(("grp", "blk"), None), P(("grp", "blk"), None), P(("grp", "blk"), None)),
        out_specs=P(("grp", "blk"), None),
        check_vma=False,
    )
```

```python
import jax
import jax.numpy as jnp
from jax import lax
from jax.sharding import PartitionSpec as P

EPS = 1e-05
TAU = 0.05


def split3(x):
    hi = lax.reduce_precision(x, exponent_bits=8, mantissa_bits=7)
    rest = x - hi
    mid = lax.reduce_precision(rest, exponent_bits=8, mantissa_bits=7)
    lo = rest - mid
    return jnp.concatenate([hi, mid, lo], axis=-1).astype(jnp.bfloat16)


def join3(parts, n):
    parts = parts.astype(jnp.float32)
    return (parts[..., :n] + parts[..., n:2 * n]) + parts[..., 2 * n:3 * n]


def piece_weights(piece, lib_ext, lib_sq, feat):
    rows = piece.reshape(-1, piece.shape[-1])
    blockf = rows[:, :feat].astype(jnp.float32)
    q_sq = jnp.sum(blockf * blockf, axis=1)
    inner = lax.dot_general(
        rows, lib_ext, (((1,), (1,)), ((), ())), preferred_element_type=jnp.float32
    )
    tanimoto = inner / (q_sq[:, None] + lib_sq[None, :] - inner)
    weight = jnp.exp((tanimoto - 1.0) / TAU)
    return weight.astype(jnp.bfloat16), jnp.sum(weight, axis=1)


def swap(x, axis, mask):
    count = lax.axis_size(axis)
    return lax.ppermute(x, axis, [(i, i ^ mask) for i in range(count)])


def digit_groups(count):
    bits = []
    while (1 << len(bits)) < count:
        bits.append(1 << len(bits))
    assert (1 << len(bits)) == count
    groups = [bits[:1], bits[1:2]]
    rest = bits[2:]
    while rest:
        groups.insert(2, rest[-2:])
        rest = rest[:-2]
    return [g for g in groups if g]


def offsets(group):
    masks = [0]
    for bit in group:
        masks = masks + [m | bit for m in masks]
    return masks


def cat(parts):
    return jnp.concatenate(parts, axis=0) if len(parts) > 1 else parts[0]


def gather_rounds(packet, axis, groups, work):
    rounds = list(reversed(groups))
    pieces = [packet[None]]
    results = []
    fresh = [packet[None]]
    early, mark = None, 0
    for r, group in enumerate(rounds):
        masks = offsets(group)[1:]
        if early is None:
            got = [[swap(cat(pieces), axis, m)] for m in masks]
        else:
            rest = cat(pieces[mark:])
            got = [[head, swap(rest, axis, m)] for head, m in zip(early, masks)]
        if r + 1 < len(rounds):
            early = [swap(cat(pieces), axis, m) for m in offsets(rounds[r + 1])[1:]]
            mark = len(pieces)
        if results:
            got, results[-1] = lax.optimization_barrier((got, results[-1]))
        got = [piece for pair in got for piece in pair]
        pieces += got
        fresh += got
        results.append(work(cat(fresh)))
        fresh = []
    return cat(pieces), results


def scatter_rounds(buf, axis, groups):
    for group in groups:
        masks = offsets(group)
        total = buf[0]
        for k in range(1, len(masks)):
            total = total + swap(buf[k], axis, masks[k])
        buf = total
    return buf


def shards(queries, library, assays):
    nblk = lax.axis_size("blk")
    groups = digit_groups(nblk)
    q_dev, feat = queries.shape
    width = assays.shape[1]
    values = assays.astype(jnp.float32)
    partial = jnp.concatenate([jnp.sum(values, axis=0), jnp.sum(values * values, axis=0)])

    coded = split3(partial)
    lanes = -(-coded.shape[0] // q_dev)
    lanes += -lanes % 128
    coded = jnp.pad(coded, (0, q_dev * lanes - coded.shape[0])).reshape(q_dev, lanes)
    packet = jnp.concatenate([queries, coded], axis=1)
    lib_ext = jnp.pad(library, ((0, 0), (0, lanes)))
    lib_sq = jnp.sum(jnp.square(library.astype(jnp.float32)), axis=1)
    got, parts = gather_rounds(
        packet, "blk", groups, lambda piece: piece_weights(piece, lib_ext, lib_sq, feat)
    )
    stats = join3(got[:, :, feat:].reshape(nblk, q_dev * lanes), 2 * width)
    stats = jnp.sum(stats, axis=0)

    col_sum, col_sq = stats[:width], stats[width:]
    total = library.shape[0] * nblk
    mean = col_sum / total
    spread = col_sq / total - mean * mean
    zvals = ((values - mean) * lax.rsqrt(spread + EPS)).astype(jnp.bfloat16)

    weight_b = jnp.concatenate([p[0] for p in parts], axis=0)
    denom = jnp.concatenate([p[1] for p in parts], axis=0)
    numer = jnp.dot(weight_b, zvals, preferred_element_type=jnp.float32)
    den = jnp.broadcast_to(denom[:, None], (denom.shape[0], 128))
    sums = jnp.concatenate([numer, den], axis=1).reshape(nblk, q_dev, width + 128)
    sums = sums.reshape(tuple(len(offsets(g)) for g in groups) + sums.shape[1:])
    mine = scatter_rounds(sums, "blk", groups)
    return mine[:, :width] / mine[:, width:width + 1]


def solution(mesh):
    return jax.shard_map(
        shards,
        mesh=mesh,
        in_specs=(P(("grp", "blk"), None), P(("grp", "blk"), None), P(("grp", "blk"), None)),
        out_specs=P(("grp", "blk"), None),
        check_vma=False,
    )
```

```python
import jax
import jax.numpy as jnp
from jax import lax
from jax.sharding import PartitionSpec as P

EPS = 1e-05
TAU = 0.05


def split3(x):
    hi = lax.reduce_precision(x, exponent_bits=8, mantissa_bits=7)
    rest = x - hi
    mid = lax.reduce_precision(rest, exponent_bits=8, mantissa_bits=7)
    lo = rest - mid
    return jnp.concatenate([hi, mid, lo], axis=-1).astype(jnp.bfloat16)


def join3(parts, n):
    parts = parts.astype(jnp.float32)
    return (parts[..., :n] + parts[..., n:2 * n]) + parts[..., 2 * n:3 * n]


def piece_weights(piece, lib_ext, lib_sq, feat):
    rows = piece.reshape(-1, piece.shape[-1])
    blockf = rows[:, :feat].astype(jnp.float32)
    q_sq = jnp.sum(blockf * blockf, axis=1)
    inner = lax.dot_general(
        lib_ext, rows, (((1,), (1,)), ((), ())), preferred_element_type=jnp.float32
    )
    tanimoto = inner / (q_sq[None, :] + lib_sq[:, None] - inner)
    weight = jnp.exp((tanimoto - 1.0) / TAU)
    return weight.astype(jnp.bfloat16), jnp.sum(weight, axis=0)


def swap(x, axis, mask):
    count = lax.axis_size(axis)
    return lax.ppermute(x, axis, [(i, i ^ mask) for i in range(count)])


def digit_groups(count):
    bits = []
    while (1 << len(bits)) < count:
        bits.append(1 << len(bits))
    assert (1 << len(bits)) == count
    groups = [bits[:1], bits[1:2]]
    rest = bits[2:]
    while rest:
        groups.insert(2, rest[-2:])
        rest = rest[:-2]
    return [g for g in groups if g]


def offsets(group):
    masks = [0]
    for bit in group:
        masks = masks + [m | bit for m in masks]
    return masks


def cat(parts):
    return jnp.concatenate(parts, axis=0) if len(parts) > 1 else parts[0]


def gather_rounds(packet, axis, groups, work):
    rounds = list(reversed(groups))
    pieces = [packet[None]]
    results = []
    fresh = [packet[None]]
    early, mark = None, 0
    for r, group in enumerate(rounds):
        masks = offsets(group)[1:]
        if early is None:
            got = [[swap(cat(pieces), axis, m)] for m in masks]
        else:
            rest = cat(pieces[mark:])
            got = [[head, swap(rest, axis, m)] for head, m in zip(early, masks)]
        if r + 1 < len(rounds):
            early = [swap(cat(pieces), axis, m) for m in offsets(rounds[r + 1])[1:]]
            mark = len(pieces)
        if results:
            got, results[-1] = lax.optimization_barrier((got, results[-1]))
        got = [piece for pair in got for piece in pair]
        pieces += got
        fresh += got
        results.append(work(cat(fresh)))
        fresh = []
    return cat(pieces), results


def scatter_rounds(buf, axis, groups):
    for group in groups:
        masks = offsets(group)
        total = buf[0]
        for k in range(1, len(masks)):
            total = total + swap(buf[k], axis, masks[k])
        buf = total
    return buf


def shards(queries, library, assays):
    nblk = lax.axis_size("blk")
    groups = digit_groups(nblk)
    q_dev, feat = queries.shape
    width = assays.shape[1]
    values = assays.astype(jnp.float32)
    partial = jnp.concatenate([jnp.sum(values, axis=0), jnp.sum(values * values, axis=0)])

    coded = split3(partial)
    lanes = -(-coded.shape[0] // q_dev)
    lanes += -lanes % 128
    coded = jnp.pad(coded, (0, q_dev * lanes - coded.shape[0])).reshape(q_dev, lanes)
    packet = jnp.concatenate([queries, coded], axis=1)
    lib_ext = jnp.pad(library, ((0, 0), (0, lanes)))
    lib_sq = jnp.sum(jnp.square(library.astype(jnp.float32)), axis=1)
    got, parts = gather_rounds(
        packet, "blk", groups, lambda piece: piece_weights(piece, lib_ext, lib_sq, feat)
    )
    stats = join3(got[:, :, feat:].reshape(nblk, q_dev * lanes), 2 * width)
    stats = jnp.sum(stats, axis=0)

    col_sum, col_sq = stats[:width], stats[width:]
    total = library.shape[0] * nblk
    mean = col_sum / total
    spread = col_sq / total - mean * mean
    zvals = ((values - mean) * lax.rsqrt(spread + EPS)).astype(jnp.bfloat16)

    weight_b = jnp.concatenate([p[0] for p in parts], axis=1)
    denom = jnp.concatenate([p[1] for p in parts], axis=0)
    numer = lax.dot_general(
        weight_b, zvals, (((0,), (0,)), ((), ())), preferred_element_type=jnp.float32
    )
    den = jnp.broadcast_to(denom[:, None], (denom.shape[0], 128))
    sums = jnp.concatenate([numer, den], axis=1).reshape(nblk, q_dev, width + 128)
    sums = sums.reshape(tuple(len(offsets(g)) for g in groups) + sums.shape[1:])
    mine = scatter_rounds(sums, "blk", groups)
    return mine[:, :width] / mine[:, width:width + 1]


def solution(mesh):
    return jax.shard_map(
        shards,
        mesh=mesh,
        in_specs=(P(("grp", "blk"), None), P(("grp", "blk"), None), P(("grp", "blk"), None)),
        out_specs=P(("grp", "blk"), None),
        check_vma=False,
    )
```

```python
import jax
import jax.numpy as jnp
from jax import lax
from jax.sharding import PartitionSpec as P

EPS = 1e-05
TAU = 0.05


def split3(x):
    hi = lax.reduce_precision(x, exponent_bits=8, mantissa_bits=7)
    rest = x - hi
    mid = lax.reduce_precision(rest, exponent_bits=8, mantissa_bits=7)
    lo = rest - mid
    return jnp.concatenate([hi, mid, lo], axis=-1).astype(jnp.bfloat16)


def join3(parts, n):
    parts = parts.astype(jnp.float32)
    return (parts[..., :n] + parts[..., n:2 * n]) + parts[..., 2 * n:3 * n]


def piece_weights(piece, libs, lib_sqs, feat):
    rows = piece.reshape(-1, piece.shape[-1])
    blockf = rows[:, :feat].astype(jnp.float32)
    q_sq = jnp.sum(blockf * blockf, axis=1)
    out, denom = [], 0.0
    for lib_ext, lib_sq in zip(libs, lib_sqs):
        inner = lax.dot_general(
            rows, lib_ext, (((1,), (1,)), ((), ())), preferred_element_type=jnp.float32
        )
        tanimoto = inner / (q_sq[:, None] + lib_sq[None, :] - inner)
        weight = jnp.exp((tanimoto - 1.0) / TAU)
        out.append(weight.astype(jnp.bfloat16))
        denom = denom + jnp.sum(weight, axis=1)
    return out, denom


def swap(x, axis, mask):
    count = lax.axis_size(axis)
    return lax.ppermute(x, axis, [(i, i ^ mask) for i in range(count)])


def digit_groups(count):
    bits = []
    while (1 << len(bits)) < count:
        bits.append(1 << len(bits))
    assert (1 << len(bits)) == count
    groups = [bits[:1], bits[1:2]]
    rest = bits[2:]
    while rest:
        groups.insert(2, rest[-2:])
        rest = rest[:-2]
    return [g for g in groups if g]


def offsets(group):
    masks = [0]
    for bit in group:
        masks = masks + [m | bit for m in masks]
    return masks


def cat(parts):
    return jnp.concatenate(parts, axis=0) if len(parts) > 1 else parts[0]


def gather_rounds(packet, axis, groups, work):
    rounds = list(reversed(groups))
    pieces = [packet[None]]
    results = []
    fresh = [packet[None]]
    early, mark = None, 0
    for r, group in enumerate(rounds):
        masks = offsets(group)[1:]
        if early is None:
            got = [[swap(cat(pieces), axis, m)] for m in masks]
        else:
            rest = cat(pieces[mark:])
            got = [[head, swap(rest, axis, m)] for head, m in zip(early, masks)]
        if r + 1 < len(rounds):
            early = [swap(cat(pieces), axis, m) for m in offsets(rounds[r + 1])[1:]]
            mark = len(pieces)
        if results:
            got, results[-1] = lax.optimization_barrier((got, results[-1]))
        got = [piece for pair in got for piece in pair]
        pieces += got
        fresh += got
        results.append(work(cat(fresh)))
        fresh = []
    return cat(pieces), results


def scatter_rounds(buf, axis, groups):
    for group in groups:
        masks = offsets(group)
        total = buf[0]
        for k in range(1, len(masks)):
            total = total + swap(buf[k], axis, masks[k])
        buf = total
    return buf


def shards(queries, library, assays):
    nblk = lax.axis_size("blk")
    groups = digit_groups(nblk)
    core, groups = groups[0][0], groups[1:]
    lineage = nblk // 2
    q_dev, feat = queries.shape
    width = assays.shape[1]
    values = assays.astype(jnp.float32)
    partial = jnp.concatenate([jnp.sum(values, axis=0), jnp.sum(values * values, axis=0)])

    partial = partial + swap(partial, "blk", core)
    pair_lib = swap(library, "blk", core)
    pair_values = swap(assays, "blk", core).astype(jnp.float32)

    coded = split3(partial)
    lanes = -(-coded.shape[0] // q_dev)
    lanes += -lanes % 128
    coded = jnp.pad(coded, (0, q_dev * lanes - coded.shape[0])).reshape(q_dev, lanes)
    packet = jnp.concatenate([queries, coded], axis=1)
    libs = [jnp.pad(lib, ((0, 0), (0, lanes))) for lib in (library, pair_lib)]
    lib_sqs = [jnp.sum(jnp.square(lib.astype(jnp.float32)), axis=1) for lib in (library, pair_lib)]
    got, parts = gather_rounds(
        packet, "blk", groups, lambda piece: piece_weights(piece, libs, lib_sqs, feat)
    )
    stats = join3(got[:, :, feat:].reshape(lineage, q_dev * lanes), 2 * width)
    stats = jnp.sum(stats, axis=0)

    col_sum, col_sq = stats[:width], stats[width:]
    total = library.shape[0] * nblk
    mean = col_sum / total
    spread = col_sq / total - mean * mean
    scale = lax.rsqrt(spread + EPS)
    numer = 0.0
    for k, vals in enumerate((values, pair_values)):
        zvals = ((vals - mean) * scale).astype(jnp.bfloat16)
        weight_b = jnp.concatenate([p[0][k] for p in parts], axis=0)
        numer = numer + jnp.dot(weight_b, zvals, preferred_element_type=jnp.float32)
    denom = jnp.concatenate([p[1] for p in parts], axis=0)
    den = jnp.broadcast_to(denom[:, None], (denom.shape[0], 128))
    sums = jnp.concatenate([numer, den], axis=1).reshape(lineage, q_dev, width + 128)
    sums = sums.reshape(tuple(len(offsets(g)) for g in groups) + sums.shape[1:])
    mine = scatter_rounds(sums, "blk", groups)
    return mine[:, :width] / mine[:, width:width + 1]


def solution(mesh):
    return jax.shard_map(
        shards,
        mesh=mesh,
        in_specs=(P(("grp", "blk"), None), P(("grp", "blk"), None), P(("grp", "blk"), None)),
        out_specs=P(("grp", "blk"), None),
        check_vma=False,
    )
```

```python
import jax
import jax.numpy as jnp
from jax import lax
from jax.sharding import PartitionSpec as P

EPS = 1e-05
TAU = 0.05


def split3(x):
    hi = lax.reduce_precision(x, exponent_bits=8, mantissa_bits=7)
    rest = x - hi
    mid = lax.reduce_precision(rest, exponent_bits=8, mantissa_bits=7)
    lo = rest - mid
    return jnp.concatenate([hi, mid, lo], axis=-1).astype(jnp.bfloat16)


def join3(parts, n):
    parts = parts.astype(jnp.float32)
    return (parts[..., :n] + parts[..., n:2 * n]) + parts[..., 2 * n:3 * n]


def piece_weights(piece, libs, lib_sqs, feat):
    rows = piece.reshape(-1, piece.shape[-1])
    blockf = rows[:, :feat].astype(jnp.float32)
    q_sq = jnp.sum(blockf * blockf, axis=1)
    out, denom = [], 0.0
    for lib_ext, lib_sq in zip(libs, lib_sqs):
        inner = lax.dot_general(
            rows, lib_ext, (((1,), (1,)), ((), ())), preferred_element_type=jnp.float32
        )
        tanimoto = inner / (q_sq[:, None] + lib_sq[None, :] - inner)
        weight = jnp.exp((tanimoto - 1.0) / TAU)
        out.append(weight.astype(jnp.bfloat16))
        denom = denom + jnp.sum(weight, axis=1)
    return out, denom


def swap(x, axis, mask):
    count = lax.axis_size(axis)
    return lax.ppermute(x, axis, [(i, i ^ mask) for i in range(count)])


def digit_groups(count):
    bits = []
    while (1 << len(bits)) < count:
        bits.append(1 << len(bits))
    assert (1 << len(bits)) == count
    groups = [bits[:1], bits[1:2]]
    rest = bits[2:]
    while rest:
        groups.insert(2, rest[-2:])
        rest = rest[:-2]
    return [g for g in groups if g]


def offsets(group):
    masks = [0]
    for bit in group:
        masks = masks + [m | bit for m in masks]
    return masks


def cat(parts):
    return jnp.concatenate(parts, axis=0) if len(parts) > 1 else parts[0]


def gather_rounds(packet, axis, groups, work):
    rounds = list(reversed(groups))
    pieces = [packet[None]]
    results = []
    fresh = [packet[None]]
    early, mark = None, 0
    for r, group in enumerate(rounds):
        masks = offsets(group)[1:]
        if early is None:
            got = [[swap(cat(pieces), axis, m)] for m in masks]
        else:
            rest = cat(pieces[mark:])
            got = [[head, swap(rest, axis, m)] for head, m in zip(early, masks)]
        if r + 1 < len(rounds):
            early = [swap(cat(pieces), axis, m) for m in offsets(rounds[r + 1])[1:]]
            mark = len(pieces)
        if results:
            got, results[-1] = lax.optimization_barrier((got, results[-1]))
        got = [piece for pair in got for piece in pair]
        pieces += got
        fresh += got
        results.append(work(cat(fresh)))
        fresh = []
    return cat(pieces), results


def scatter_rounds(buf, axis, groups):
    for group in groups:
        masks = offsets(group)
        total = buf[0]
        for k in range(1, len(masks)):
            total = total + swap(buf[k], axis, masks[k])
        buf = total
    return buf


def shards(queries, library, assays):
    nblk = lax.axis_size("blk")
    groups = digit_groups(nblk)
    core, groups = groups[0][0], groups[1:]
    lineage = nblk // 2
    q_dev, feat = queries.shape
    width = assays.shape[1]
    values = assays.astype(jnp.float32)
    partial = jnp.concatenate([jnp.sum(values, axis=0), jnp.sum(values * values, axis=0)])

    partial = partial + swap(partial, "blk", core)
    pair_lib = swap(library, "blk", core)
    pair_values = swap(assays, "blk", core).astype(jnp.float32)

    coded = split3(partial)
    lanes = -(-coded.shape[0] // q_dev)
    lanes += -lanes % 128
    coded = jnp.pad(coded, (0, q_dev * lanes - coded.shape[0])).reshape(q_dev, lanes)
    packet = jnp.concatenate([queries, coded], axis=1)
    chip_lib = jnp.concatenate([library, pair_lib], axis=0)
    libs = [jnp.pad(chip_lib, ((0, 0), (0, lanes)))]
    lib_sqs = [jnp.sum(jnp.square(chip_lib.astype(jnp.float32)), axis=1)]
    got, parts = gather_rounds(
        packet, "blk", groups, lambda piece: piece_weights(piece, libs, lib_sqs, feat)
    )
    stats = join3(got[:, :, feat:].reshape(lineage, q_dev * lanes), 2 * width)
    stats = jnp.sum(stats, axis=0)

    col_sum, col_sq = stats[:width], stats[width:]
    total = library.shape[0] * nblk
    mean = col_sum / total
    spread = col_sq / total - mean * mean
    scale = lax.rsqrt(spread + EPS)
    chip_values = jnp.concatenate([values, pair_values], axis=0)
    zvals = ((chip_values - mean) * scale).astype(jnp.bfloat16)
    weight_b = jnp.concatenate([p[0][0] for p in parts], axis=0)
    numer = jnp.dot(weight_b, zvals, preferred_element_type=jnp.float32)
    denom = jnp.concatenate([p[1] for p in parts], axis=0)
    den = jnp.broadcast_to(denom[:, None], (denom.shape[0], 128))
    sums = jnp.concatenate([numer, den], axis=1).reshape(lineage, q_dev, width + 128)
    sums = sums.reshape(tuple(len(offsets(g)) for g in groups) + sums.shape[1:])
    mine = scatter_rounds(sums, "blk", groups)
    return mine[:, :width] / mine[:, width:width + 1]


def solution(mesh):
    return jax.shard_map(
        shards,
        mesh=mesh,
        in_specs=(P(("grp", "blk"), None), P(("grp", "blk"), None), P(("grp", "blk"), None)),
        out_specs=P(("grp", "blk"), None),
        check_vma=False,
    )
```

```python
import jax
import jax.numpy as jnp
from jax import lax
from jax.sharding import PartitionSpec as P

EPS = 1e-05
TAU = 0.05


def split3(x):
    hi = lax.reduce_precision(x, exponent_bits=8, mantissa_bits=7)
    rest = x - hi
    mid = lax.reduce_precision(rest, exponent_bits=8, mantissa_bits=7)
    lo = rest - mid
    return jnp.concatenate([hi, mid, lo], axis=-1).astype(jnp.bfloat16)


def join3(parts, n):
    parts = parts.astype(jnp.float32)
    return (parts[..., :n] + parts[..., n:2 * n]) + parts[..., 2 * n:3 * n]


def piece_weights(piece, libs, lib_sqs, feat):
    rows = piece.reshape(-1, piece.shape[-1])
    blockf = rows[:, :feat].astype(jnp.float32)
    q_sq = jnp.sum(blockf * blockf, axis=1)
    out, denom = [], 0.0
    for lib_ext, lib_sq in zip(libs, lib_sqs):
        inner = lax.dot_general(
            rows, lib_ext, (((1,), (1,)), ((), ())), preferred_element_type=jnp.float32
        )
        tanimoto = inner / (q_sq[:, None] + lib_sq[None, :] - inner)
        weight = jnp.exp((tanimoto - 1.0) / TAU)
        out.append(weight.astype(jnp.bfloat16))
        denom = denom + jnp.sum(weight, axis=1)
    return out, denom


def swap(x, axis, mask):
    count = lax.axis_size(axis)
    return lax.ppermute(x, axis, [(i, i ^ mask) for i in range(count)])


def digit_groups(count):
    bits = []
    while (1 << len(bits)) < count:
        bits.append(1 << len(bits))
    assert (1 << len(bits)) == count
    groups = [bits[:1], bits[1:2]]
    rest = bits[2:]
    while rest:
        groups.insert(2, rest[-2:])
        rest = rest[:-2]
    return [g for g in groups if g]


def offsets(group):
    masks = [0]
    for bit in group:
        masks = masks + [m | bit for m in masks]
    return masks


def cat(parts):
    return jnp.concatenate(parts, axis=0) if len(parts) > 1 else parts[0]


def gather_rounds(packet, axis, groups, work):
    rounds = list(reversed(groups))
    pieces = [packet[None]]
    results = []
    fresh = [packet[None]]
    early, mark = None, 0
    for r, group in enumerate(rounds):
        masks = offsets(group)[1:]
        if early is None:
            got = [[swap(cat(pieces), axis, m)] for m in masks]
        else:
            rest = cat(pieces[mark:])
            got = [[head, swap(rest, axis, m)] for head, m in zip(early, masks)]
        if r + 1 < len(rounds):
            early = [swap(cat(pieces), axis, m) for m in offsets(rounds[r + 1])[1:]]
            mark = len(pieces)
        if results:
            got, results[-1] = lax.optimization_barrier((got, results[-1]))
        got = [piece for pair in got for piece in pair]
        pieces += got
        fresh += got
        results.append(work(cat(fresh)))
        fresh = []
    return cat(pieces), results


def scatter_rounds(buf, axis, groups):
    for group in groups:
        masks = offsets(group)
        total = buf[0]
        for k in range(1, len(masks)):
            total = total + swap(buf[k], axis, masks[k])
        buf = total
    return buf


def shards(queries, library, assays):
    nblk = lax.axis_size("blk")
    groups = digit_groups(nblk)
    core, groups = groups[0][0], groups[1:]
    lineage = nblk // 2
    q_dev, feat = queries.shape
    width = assays.shape[1]
    values = assays.astype(jnp.float32)
    partial = jnp.concatenate([jnp.sum(values, axis=0), jnp.sum(values * values, axis=0)])

    pair_lib = swap(library, "blk", core)
    pair_values = swap(assays, "blk", core).astype(jnp.float32)

    coded = split3(partial)
    lanes = -(-coded.shape[0] // q_dev)
    lanes += -lanes % 128
    coded = jnp.pad(coded, (0, q_dev * lanes - coded.shape[0])).reshape(q_dev, lanes)
    packet = jnp.concatenate([queries, coded], axis=1)
    libs = [jnp.pad(lib, ((0, 0), (0, lanes))) for lib in (library, pair_lib)]
    lib_sqs = [jnp.sum(jnp.square(lib.astype(jnp.float32)), axis=1) for lib in (library, pair_lib)]
    got, parts = gather_rounds(
        packet, "blk", groups, lambda piece: piece_weights(piece, libs, lib_sqs, feat)
    )
    stats = join3(got[:, :, feat:].reshape(lineage, q_dev * lanes), 2 * width)
    stats = jnp.sum(stats, axis=0)
    stats = stats + swap(stats, "blk", core)

    col_sum, col_sq = stats[:width], stats[width:]
    total = library.shape[0] * nblk
    mean = col_sum / total
    spread = col_sq / total - mean * mean
    scale = lax.rsqrt(spread + EPS)
    numer = 0.0
    for k, vals in enumerate((values, pair_values)):
        zvals = ((vals - mean) * scale).astype(jnp.bfloat16)
        weight_b = jnp.concatenate([p[0][k] for p in parts], axis=0)
        numer = numer + jnp.dot(weight_b, zvals, preferred_element_type=jnp.float32)
    denom = jnp.concatenate([p[1] for p in parts], axis=0)
    den = jnp.broadcast_to(denom[:, None], (denom.shape[0], 128))
    sums = jnp.concatenate([numer, den], axis=1).reshape(lineage, q_dev, width + 128)
    sums = sums.reshape(tuple(len(offsets(g)) for g in groups) + sums.shape[1:])
    mine = scatter_rounds(sums, "blk", groups)
    return mine[:, :width] / mine[:, width:width + 1]


def solution(mesh):
    return jax.shard_map(
        shards,
        mesh=mesh,
        in_specs=(P(("grp", "blk"), None), P(("grp", "blk"), None), P(("grp", "blk"), None)),
        out_specs=P(("grp", "blk"), None),
        check_vma=False,
    )
```

```python
import jax
import jax.numpy as jnp
from jax import lax
from jax.sharding import PartitionSpec as P

EPS = 1e-05
TAU = 0.05


def split3(x):
    hi = lax.reduce_precision(x, exponent_bits=8, mantissa_bits=7)
    rest = x - hi
    mid = lax.reduce_precision(rest, exponent_bits=8, mantissa_bits=7)
    lo = rest - mid
    return jnp.concatenate([hi, mid, lo], axis=-1).astype(jnp.bfloat16)


def join3(parts, n):
    parts = parts.astype(jnp.float32)
    return (parts[..., :n] + parts[..., n:2 * n]) + parts[..., 2 * n:3 * n]


def piece_weights(piece, libs, lib_sqs, feat):
    rows = piece.reshape(-1, piece.shape[-1])
    blockf = rows[:, :feat].astype(jnp.float32)
    q_sq = jnp.sum(blockf * blockf, axis=1)
    out, denom = [], 0.0
    for lib_ext, lib_sq in zip(libs, lib_sqs):
        inner = lax.dot_general(
            rows, lib_ext, (((1,), (1,)), ((), ())), preferred_element_type=jnp.float32
        )
        tanimoto = inner / (q_sq[:, None] + lib_sq[None, :] - inner)
        weight = jnp.exp((tanimoto - 1.0) / TAU)
        out.append(weight.astype(jnp.bfloat16))
        denom = denom + jnp.sum(weight, axis=1)
    return out, denom


def swap(x, axis, mask):
    count = lax.axis_size(axis)
    return lax.ppermute(x, axis, [(i, i ^ mask) for i in range(count)])


def digit_groups(count):
    bits = []
    while (1 << len(bits)) < count:
        bits.append(1 << len(bits))
    assert (1 << len(bits)) == count
    groups = [bits[:1], bits[1:2]]
    rest = bits[2:]
    while rest:
        groups.insert(2, rest[-2:])
        rest = rest[:-2]
    return [g for g in groups if g]


def offsets(group):
    masks = [0]
    for bit in group:
        masks = masks + [m | bit for m in masks]
    return masks


def cat(parts):
    return jnp.concatenate(parts, axis=0) if len(parts) > 1 else parts[0]


def gather_rounds(packet, axis, groups, work):
    rounds = list(reversed(groups))
    pieces = [packet[None]]
    results = []
    fresh = [packet[None]]
    early, mark = None, 0
    for r, group in enumerate(rounds):
        masks = offsets(group)[1:]
        if early is None:
            got = [[swap(cat(pieces), axis, m)] for m in masks]
        else:
            rest = cat(pieces[mark:])
            got = [[head, swap(rest, axis, m)] for head, m in zip(early, masks)]
        if r + 1 < len(rounds):
            early = [swap(cat(pieces), axis, m) for m in offsets(rounds[r + 1])[1:]]
            mark = len(pieces)
        if results:
            got, results[-1] = lax.optimization_barrier((got, results[-1]))
        got = [piece for pair in got for piece in pair]
        pieces += got
        fresh += got
        results.append(work(cat(fresh)))
        fresh = []
    return cat(pieces), results


def scatter_rounds(buf, axis, groups):
    for group in groups:
        masks = offsets(group)
        total = buf[0]
        for k in range(1, len(masks)):
            total = total + swap(buf[k], axis, masks[k])
        buf = total
    return buf


def shards(queries, library, assays):
    nblk = lax.axis_size("blk")
    groups = digit_groups(nblk)
    core, groups = groups[0][0], groups[1:]
    lineage = nblk // 2
    q_dev, feat = queries.shape
    width = assays.shape[1]
    values = assays.astype(jnp.float32)
    partial = jnp.concatenate([jnp.sum(values, axis=0), jnp.sum(values * values, axis=0)])

    pair_lib = swap(library, "blk", core)
    pair_values = swap(assays, "blk", core).astype(jnp.float32)

    coded = split3(partial)
    lanes = -(-coded.shape[0] // q_dev)
    lanes += -lanes % 128
    coded = jnp.pad(coded, (0, q_dev * lanes - coded.shape[0])).reshape(q_dev, lanes)
    packet = jnp.concatenate([queries, coded], axis=1)
    libs = [jnp.pad(lib, ((0, 0), (0, lanes))) for lib in (library, pair_lib)]
    lib_sqs = [jnp.sum(jnp.square(lib.astype(jnp.float32)), axis=1) for lib in (library, pair_lib)]
    got, parts = gather_rounds(
        packet, "blk", groups, lambda piece: piece_weights(piece, libs, lib_sqs, feat)
    )
    stats = join3(got[:, :, feat:].reshape(lineage, q_dev * lanes), 2 * width)
    stats = jnp.sum(stats, axis=0)
    stats = stats + swap(stats, "blk", core)

    col_sum, col_sq = stats[:width], stats[width:]
    total = library.shape[0] * nblk
    mean = col_sum / total
    spread = col_sq / total - mean * mean
    scale = lax.rsqrt(spread + EPS)
    numer = 0.0
    for k, vals in enumerate((values, pair_values)):
        zvals = ((vals - mean) * scale).astype(jnp.bfloat16)
        weight_b = jnp.concatenate([p[0][k] for p in parts], axis=0)
        numer = numer + jnp.dot(weight_b, zvals, preferred_element_type=jnp.float32)
    denom = jnp.concatenate([p[1] for p in parts], axis=0)
    den = jnp.broadcast_to(denom[:, None], (denom.shape[0], 128))
    sums = jnp.concatenate([numer, den], axis=1).reshape(lineage, q_dev, width + 128)
    sums = sums.reshape(tuple(len(offsets(g)) for g in groups) + sums.shape[1:])
    order = list(range(1, len(groups))) + [0]
    sums = jnp.transpose(sums, order + list(range(len(groups), sums.ndim)))
    mine = scatter_rounds(sums, "blk", [groups[k] for k in order])
    return mine[:, :width] / mine[:, width:width + 1]


def solution(mesh):
    return jax.shard_map(
        shards,
        mesh=mesh,
        in_specs=(P(("grp", "blk"), None), P(("grp", "blk"), None), P(("grp", "blk"), None)),
        out_specs=P(("grp", "blk"), None),
        check_vma=False,
    )
```

```python
import jax
import jax.numpy as jnp
from jax import lax
from jax.sharding import PartitionSpec as P

EPS = 1e-05
TAU = 0.05


def split3(x):
    hi = lax.reduce_precision(x, exponent_bits=8, mantissa_bits=7)
    rest = x - hi
    mid = lax.reduce_precision(rest, exponent_bits=8, mantissa_bits=7)
    lo = rest - mid
    return jnp.concatenate([hi, mid, lo], axis=-1).astype(jnp.bfloat16)


def join3(parts, n):
    parts = parts.astype(jnp.float32)
    return (parts[..., :n] + parts[..., n:2 * n]) + parts[..., 2 * n:3 * n]


def piece_weights(piece, libs, lib_sqs, feat):
    rows = piece.reshape(-1, piece.shape[-1])
    blockf = rows[:, :feat].astype(jnp.float32)
    q_sq = jnp.sum(blockf * blockf, axis=1)
    out, denom = [], 0.0
    for lib_ext, lib_sq in zip(libs, lib_sqs):
        inner = lax.dot_general(
            rows, lib_ext, (((1,), (1,)), ((), ())), preferred_element_type=jnp.float32
        )
        tanimoto = inner / (q_sq[:, None] + lib_sq[None, :] - inner)
        weight = jnp.exp((tanimoto - 1.0) / TAU)
        out.append(weight.astype(jnp.bfloat16))
        denom = denom + jnp.sum(weight, axis=1)
    return out, denom


def swap(x, axis, mask):
    count = lax.axis_size(axis)
    return lax.ppermute(x, axis, [(i, i ^ mask) for i in range(count)])


def digit_groups(count):
    bits = []
    while (1 << len(bits)) < count:
        bits.append(1 << len(bits))
    assert (1 << len(bits)) == count
    groups = [bits[:1], bits[1:2]]
    rest = bits[2:]
    while rest:
        groups.insert(2, rest[-2:])
        rest = rest[:-2]
    return [g for g in groups if g]


def offsets(group):
    masks = [0]
    for bit in group:
        masks = masks + [m | bit for m in masks]
    return masks


def cat(parts):
    return jnp.concatenate(parts, axis=0) if len(parts) > 1 else parts[0]


def gather_rounds(packet, axis, groups, work):
    rounds = list(reversed(groups))
    pieces = [packet[None]]
    results = []
    fresh = [packet[None]]
    early, mark = None, 0
    for r, group in enumerate(rounds):
        masks = offsets(group)[1:]
        if early is None:
            got = [[swap(cat(pieces), axis, m)] for m in masks]
        else:
            rest = cat(pieces[mark:])
            got = [[head, swap(rest, axis, m)] for head, m in zip(early, masks)]
        if r + 1 < len(rounds):
            early = [swap(cat(pieces), axis, m) for m in offsets(rounds[r + 1])[1:]]
            mark = len(pieces)
        if results:
            got, results[-1] = lax.optimization_barrier((got, results[-1]))
        got = [piece for pair in got for piece in pair]
        pieces += got
        fresh += got
        results.append(work(cat(fresh)))
        fresh = []
    return cat(pieces), results


def scatter_rounds(buf, axis, groups):
    for group in groups:
        masks = offsets(group)
        total = buf[0]
        for k in range(1, len(masks)):
            total = total + swap(buf[k], axis, masks[k])
        buf = total
    return buf


def shards(queries, library, assays):
    nblk = lax.axis_size("blk")
    groups = digit_groups(nblk)
    core, groups = groups[0][0], groups[1:]
    lineage = nblk // 2
    q_dev, feat = queries.shape
    width = assays.shape[1]
    values = assays.astype(jnp.float32)
    partial = jnp.concatenate([jnp.sum(values, axis=0), jnp.sum(values * values, axis=0)])

    coded = split3(partial)
    lanes = -(-coded.shape[0] // q_dev)
    lanes += -lanes % 128
    coded = jnp.pad(coded, (0, q_dev * lanes - coded.shape[0])).reshape(q_dev, lanes)
    packet = jnp.concatenate([queries, coded], axis=1)
    packet, held = lax.optimization_barrier((packet, library))
    pair_lib = swap(held, "blk", core)
    pair_values = swap(assays, "blk", core).astype(jnp.float32)
    libs = [jnp.pad(lib, ((0, 0), (0, lanes))) for lib in (library, pair_lib)]
    lib_sqs = [jnp.sum(jnp.square(lib.astype(jnp.float32)), axis=1) for lib in (library, pair_lib)]
    got, parts = gather_rounds(
        packet, "blk", groups, lambda piece: piece_weights(piece, libs, lib_sqs, feat)
    )
    stats = join3(got[:, :, feat:].reshape(lineage, q_dev * lanes), 2 * width)
    stats = jnp.sum(stats, axis=0)
    stats = stats + swap(stats, "blk", core)

    col_sum, col_sq = stats[:width], stats[width:]
    total = library.shape[0] * nblk
    mean = col_sum / total
    spread = col_sq / total - mean * mean
    scale = lax.rsqrt(spread + EPS)
    numer = 0.0
    for k, vals in enumerate((values, pair_values)):
        zvals = ((vals - mean) * scale).astype(jnp.bfloat16)
        weight_b = jnp.concatenate([p[0][k] for p in parts], axis=0)
        numer = numer + jnp.dot(weight_b, zvals, preferred_element_type=jnp.float32)
    denom = jnp.concatenate([p[1] for p in parts], axis=0)
    den = jnp.broadcast_to(denom[:, None], (denom.shape[0], 128))
    sums = jnp.concatenate([numer, den], axis=1).reshape(lineage, q_dev, width + 128)
    sums = sums.reshape(tuple(len(offsets(g)) for g in groups) + sums.shape[1:])
    order = list(range(1, len(groups))) + [0]
    sums = jnp.transpose(sums, order + list(range(len(groups), sums.ndim)))
    mine = scatter_rounds(sums, "blk", [groups[k] for k in order])
    return mine[:, :width] / mine[:, width:width + 1]


def solution(mesh):
    return jax.shard_map(
        shards,
        mesh=mesh,
        in_specs=(P(("grp", "blk"), None), P(("grp", "blk"), None), P(("grp", "blk"), None)),
        out_specs=P(("grp", "blk"), None),
        check_vma=False,
    )
```

```python
import jax
import jax.numpy as jnp
from jax import lax
from jax.sharding import PartitionSpec as P

EPS = 1e-05
TAU = 0.05


def split3(x):
    hi = lax.reduce_precision(x, exponent_bits=8, mantissa_bits=7)
    rest = x - hi
    mid = lax.reduce_precision(rest, exponent_bits=8, mantissa_bits=7)
    lo = rest - mid
    return jnp.concatenate([hi, mid, lo], axis=-1).astype(jnp.bfloat16)


def join3(parts, n):
    parts = parts.astype(jnp.float32)
    return (parts[..., :n] + parts[..., n:2 * n]) + parts[..., 2 * n:3 * n]


def piece_weights(piece, libs, lib_sqs, feat):
    rows = piece.reshape(-1, piece.shape[-1])
    blockf = rows[:, :feat].astype(jnp.float32)
    q_sq = jnp.sum(blockf * blockf, axis=1)
    out, denom = [], 0.0
    for lib_ext, lib_sq in zip(libs, lib_sqs):
        inner = lax.dot_general(
            rows, lib_ext, (((1,), (1,)), ((), ())), preferred_element_type=jnp.float32
        )
        tanimoto = inner / (q_sq[:, None] + lib_sq[None, :] - inner)
        weight = jnp.exp((tanimoto - 1.0) / TAU)
        out.append(weight.astype(jnp.bfloat16))
        denom = denom + jnp.sum(weight, axis=1)
    return out, denom


def swap(x, axis, mask):
    count = lax.axis_size(axis)
    return lax.ppermute(x, axis, [(i, i ^ mask) for i in range(count)])


def digit_groups(count):
    bits = []
    while (1 << len(bits)) < count:
        bits.append(1 << len(bits))
    assert (1 << len(bits)) == count
    groups = [bits[:1], bits[1:2]]
    rest = bits[2:]
    while rest:
        groups.insert(2, rest[-2:])
        rest = rest[:-2]
    return [g for g in groups if g]


def offsets(group):
    masks = [0]
    for bit in group:
        masks = masks + [m | bit for m in masks]
    return masks


def cat(parts):
    return jnp.concatenate(parts, axis=0) if len(parts) > 1 else parts[0]


def gather_rounds(packet, axis, groups, work):
    rounds = list(reversed(groups))
    pieces = [packet[None]]
    results = []
    fresh = [packet[None]]
    early, mark = None, 0
    for r, group in enumerate(rounds):
        masks = offsets(group)[1:]
        if early is None:
            got = [[swap(cat(pieces), axis, m)] for m in masks]
        else:
            rest = cat(pieces[mark:])
            got = [[head, swap(rest, axis, m)] for head, m in zip(early, masks)]
        if r + 1 < len(rounds):
            early = [swap(cat(pieces), axis, m) for m in offsets(rounds[r + 1])[1:]]
            mark = len(pieces)
        if results:
            got, results[-1] = lax.optimization_barrier((got, results[-1]))
        got = [piece for pair in got for piece in pair]
        pieces += got
        fresh += got
        results.append(work(cat(fresh)))
        fresh = []
    return cat(pieces), results


def scatter_rounds(buf, axis, groups):
    for group in groups:
        masks = offsets(group)
        total = buf[0]
        for k in range(1, len(masks)):
            total = total + swap(buf[k], axis, masks[k])
        buf = total
    return buf


def shards(queries, library, assays):
    nblk = lax.axis_size("blk")
    groups = digit_groups(nblk)
    core, groups = groups[0][0], groups[1:]
    lineage = nblk // 2
    q_dev, feat = queries.shape
    width = assays.shape[1]
    values = assays.astype(jnp.float32)
    partial = jnp.concatenate([jnp.sum(values, axis=0), jnp.sum(values * values, axis=0)])

    pair_lib = swap(library, "blk", core)
    pair_values = swap(assays, "blk", core).astype(jnp.float32)

    coded = split3(partial)
    lanes = -(-coded.shape[0] // q_dev)
    lanes += -lanes % 128
    coded = jnp.pad(coded, (0, q_dev * lanes - coded.shape[0])).reshape(q_dev, lanes)
    packet = jnp.concatenate([queries, coded], axis=1)
    libs = [jnp.pad(lib, ((0, 0), (0, lanes))) for lib in (library, pair_lib)]
    lib_sqs = [jnp.sum(jnp.square(lib.astype(jnp.float32)), axis=1) for lib in (library, pair_lib)]
    got, parts = gather_rounds(
        packet, "blk", groups, lambda piece: piece_weights(piece, libs, lib_sqs, feat)
    )
    stats = join3(got[:, :, feat:].reshape(lineage, q_dev * lanes), 2 * width)
    stats = jnp.sum(stats, axis=0)
    stats = stats + swap(stats, "blk", core)

    col_sum, col_sq = stats[:width], stats[width:]
    total = library.shape[0] * nblk
    mean = col_sum / total
    spread = col_sq / total - mean * mean
    scale = lax.rsqrt(spread + EPS)
    numer = 0.0
    for k, vals in enumerate((values, pair_values)):
        zvals = ((vals - mean) * scale).astype(jnp.bfloat16)
        weight_b = jnp.concatenate([p[0][k] for p in parts], axis=0)
        numer = numer + jnp.dot(weight_b, zvals, preferred_element_type=jnp.float32)
    denom = jnp.concatenate([p[1] for p in parts], axis=0)
    den = jnp.broadcast_to(denom[:, None], (denom.shape[0], 128))
    sums = jnp.concatenate([numer, den], axis=1).reshape(lineage, q_dev, width + 128)
    sums = sums.reshape(tuple(len(offsets(g)) for g in groups) + sums.shape[1:])
    order = list(range(1, len(groups))) + [0]
    sums = jnp.transpose(sums, order + list(range(len(groups), sums.ndim)))
    bits = [bit for k in order for bit in reversed(groups[k])]
    sums = sums.reshape((2,) * len(bits) + sums.shape[len(groups):])
    mine = scatter_rounds(sums, "blk", [[bit] for bit in bits])
    return mine[:, :width] / mine[:, width:width + 1]


def solution(mesh):
    return jax.shard_map(
        shards,
        mesh=mesh,
        in_specs=(P(("grp", "blk"), None), P(("grp", "blk"), None), P(("grp", "blk"), None)),
        out_specs=P(("grp", "blk"), None),
        check_vma=False,
    )
```

```python
import jax
import jax.numpy as jnp
from jax import lax
from jax.sharding import PartitionSpec as P

EPS = 1e-05
TAU = 0.05


def split3(x):
    hi = lax.reduce_precision(x, exponent_bits=8, mantissa_bits=7)
    rest = x - hi
    mid = lax.reduce_precision(rest, exponent_bits=8, mantissa_bits=7)
    lo = rest - mid
    return jnp.concatenate([hi, mid, lo], axis=-1).astype(jnp.bfloat16)


def join3(parts, n):
    parts = parts.astype(jnp.float32)
    return (parts[..., :n] + parts[..., n:2 * n]) + parts[..., 2 * n:3 * n]


def piece_weights(piece, libs, lib_sqs, feat):
    rows = piece.reshape(-1, piece.shape[-1])
    blockf = rows[:, :feat].astype(jnp.float32)
    q_sq = jnp.sum(blockf * blockf, axis=1)
    out, denom = [], 0.0
    for lib_ext, lib_sq in zip(libs, lib_sqs):
        inner = lax.dot_general(
            rows, lib_ext, (((1,), (1,)), ((), ())), preferred_element_type=jnp.float32
        )
        tanimoto = inner / (q_sq[:, None] + lib_sq[None, :] - inner)
        weight = jnp.exp((tanimoto - 1.0) / TAU)
        out.append(weight.astype(jnp.bfloat16))
        denom = denom + jnp.sum(weight, axis=1)
    return out, denom


def swap(x, axis, mask):
    count = lax.axis_size(axis)
    return lax.ppermute(x, axis, [(i, i ^ mask) for i in range(count)])


def digit_groups(count):
    bits = []
    while (1 << len(bits)) < count:
        bits.append(1 << len(bits))
    assert (1 << len(bits)) == count
    groups = [bits[:1], bits[1:2]]
    rest = bits[2:]
    while rest:
        groups.insert(2, rest[-2:])
        rest = rest[:-2]
    return [g for g in groups if g]


def offsets(group):
    masks = [0]
    for bit in group:
        masks = masks + [m | bit for m in masks]
    return masks


def cat(parts):
    return jnp.concatenate(parts, axis=0) if len(parts) > 1 else parts[0]


def gather_rounds(packet, axis, groups, work):
    rounds = list(reversed(groups))
    pieces = [packet[None]]
    results = []
    fresh = [packet[None]]
    early, mark = None, 0
    for r, group in enumerate(rounds):
        masks = offsets(group)[1:]
        if early is None:
            got = [[swap(cat(pieces), axis, m)] for m in masks]
        else:
            rest = cat(pieces[mark:])
            got = [[head, swap(rest, axis, m)] for head, m in zip(early, masks)]
        if r + 1 < len(rounds):
            early = [swap(cat(pieces), axis, m) for m in offsets(rounds[r + 1])[1:]]
            mark = len(pieces)
        if results:
            got, results[-1] = lax.optimization_barrier((got, results[-1]))
        got = [piece for pair in got for piece in pair]
        pieces += got
        fresh += got
        results.append(work(cat(fresh)))
        fresh = []
    return cat(pieces), results


def scatter_rounds(buf, axis, groups):
    for group in groups:
        masks = offsets(group)
        total = buf[0]
        for k in range(1, len(masks)):
            total = total + swap(buf[k], axis, masks[k])
        buf = total
    return buf


def shards(queries, library, assays):
    nblk = lax.axis_size("blk")
    groups = digit_groups(nblk)
    core, groups = groups[0][0], groups[1:]
    lineage = nblk // 2
    q_dev, feat = queries.shape
    width = assays.shape[1]
    values = assays.astype(jnp.float32)
    partial = jnp.concatenate([jnp.sum(values, axis=0), jnp.sum(values * values, axis=0)])

    pair_lib = swap(library, "blk", core)
    pair_values = swap(assays, "blk", core).astype(jnp.float32)

    coded = split3(partial)
    lanes = -(-coded.shape[0] // q_dev)
    lanes += -lanes % 128
    coded = jnp.pad(coded, (0, q_dev * lanes - coded.shape[0])).reshape(q_dev, lanes)
    packet = jnp.concatenate([queries, coded], axis=1)
    libs = [jnp.pad(lib, ((0, 0), (0, lanes))) for lib in (library, pair_lib)]
    lib_sqs = [jnp.sum(jnp.square(lib.astype(jnp.float32)), axis=1) for lib in (library, pair_lib)]
    got, parts = gather_rounds(
        packet, "blk", groups, lambda piece: piece_weights(piece, libs, lib_sqs, feat)
    )
    stats = join3(got[:, :, feat:].reshape(lineage, q_dev * lanes), 2 * width)
    stats = jnp.sum(stats, axis=0)
    stats = stats + swap(stats, "blk", core)

    col_sum, col_sq = stats[:width], stats[width:]
    total = library.shape[0] * nblk
    mean = col_sum / total
    spread = col_sq / total - mean * mean
    scale = lax.rsqrt(spread + EPS)
    zvals = jnp.concatenate(
        [((vals - mean) * scale).astype(jnp.bfloat16) for vals in (values, pair_values)], axis=0
    )
    weight_b = jnp.concatenate(
        [jnp.concatenate([p[0][k] for p in parts], axis=0) for k in range(2)], axis=1
    )
    numer = jnp.dot(weight_b, zvals, preferred_element_type=jnp.float32)
    denom = jnp.concatenate([p[1] for p in parts], axis=0)
    den = jnp.broadcast_to(denom[:, None], (denom.shape[0], 128))
    sums = jnp.concatenate([numer, den], axis=1).reshape(lineage, q_dev, width + 128)
    sums = sums.reshape(tuple(len(offsets(g)) for g in groups) + sums.shape[1:])
    order = list(range(1, len(groups))) + [0]
    sums = jnp.transpose(sums, order + list(range(len(groups), sums.ndim)))
    mine = scatter_rounds(sums, "blk", [groups[k] for k in order])
    return mine[:, :width] / mine[:, width:width + 1]


def solution(mesh):
    return jax.shard_map(
        shards,
        mesh=mesh,
        in_specs=(P(("grp", "blk"), None), P(("grp", "blk"), None), P(("grp", "blk"), None)),
        out_specs=P(("grp", "blk"), None),
        check_vma=False,
    )
```

```python
import jax
import jax.numpy as jnp
from jax import lax
from jax.sharding import PartitionSpec as P

EPS = 1e-05
TAU = 0.05


def split3(x):
    hi = lax.reduce_precision(x, exponent_bits=8, mantissa_bits=7)
    rest = x - hi
    mid = lax.reduce_precision(rest, exponent_bits=8, mantissa_bits=7)
    lo = rest - mid
    return jnp.concatenate([hi, mid, lo], axis=-1).astype(jnp.bfloat16)


def join3(parts, n):
    parts = parts.astype(jnp.float32)
    return (parts[..., :n] + parts[..., n:2 * n]) + parts[..., 2 * n:3 * n]


def piece_weights(piece, libs, lib_sqs, feat):
    rows = piece.reshape(-1, piece.shape[-1])
    blockf = rows[:, :feat].astype(jnp.float32)
    q_sq = jnp.sum(blockf * blockf, axis=1)
    out, denom = [], 0.0
    for lib_ext, lib_sq in zip(libs, lib_sqs):
        inner = lax.dot_general(
            rows, lib_ext, (((1,), (1,)), ((), ())), preferred_element_type=jnp.float32
        )
        tanimoto = inner / (q_sq[:, None] + lib_sq[None, :] - inner)
        weight = jnp.exp((tanimoto - 1.0) / TAU)
        out.append(weight.astype(jnp.bfloat16))
        denom = denom + jnp.sum(weight, axis=1)
    return out, denom


def swap(x, axis, mask):
    count = lax.axis_size(axis)
    return lax.ppermute(x, axis, [(i, i ^ mask) for i in range(count)])


def digit_groups(count):
    bits = []
    while (1 << len(bits)) < count:
        bits.append(1 << len(bits))
    assert (1 << len(bits)) == count
    groups = [bits[:1], bits[1:2]]
    rest = bits[2:]
    while rest:
        groups.insert(2, rest[-2:])
        rest = rest[:-2]
    return [g for g in groups if g]


def offsets(group):
    masks = [0]
    for bit in group:
        masks = masks + [m | bit for m in masks]
    return masks


def cat(parts):
    return jnp.concatenate(parts, axis=0) if len(parts) > 1 else parts[0]


def gather_rounds(packet, axis, groups, work):
    rounds = list(reversed(groups))
    pieces = [packet[None]]
    results = []
    fresh = [packet[None]]
    early, mark = None, 0
    for r, group in enumerate(rounds):
        masks = offsets(group)[1:]
        if early is None:
            got = [[swap(cat(pieces), axis, m)] for m in masks]
        else:
            rest = cat(pieces[mark:])
            got = [[head, swap(rest, axis, m)] for head, m in zip(early, masks)]
        if r + 1 < len(rounds):
            early = [swap(cat(pieces), axis, m) for m in offsets(rounds[r + 1])[1:]]
            mark = len(pieces)
        got = [piece for pair in got for piece in pair]
        pieces += got
        fresh += got
        results.append(work(cat(fresh)))
        fresh = []
    return cat(pieces), results


def scatter_rounds(buf, axis, groups):
    for group in groups:
        masks = offsets(group)
        total = buf[0]
        for k in range(1, len(masks)):
            total = total + swap(buf[k], axis, masks[k])
        buf = total
    return buf


def shards(queries, library, assays):
    nblk = lax.axis_size("blk")
    groups = digit_groups(nblk)
    core, groups = groups[0][0], groups[1:]
    lineage = nblk // 2
    q_dev, feat = queries.shape
    width = assays.shape[1]
    values = assays.astype(jnp.float32)
    partial = jnp.concatenate([jnp.sum(values, axis=0), jnp.sum(values * values, axis=0)])

    pair_lib = swap(library, "blk", core)
    pair_values = swap(assays, "blk", core).astype(jnp.float32)

    coded = split3(partial)
    lanes = -(-coded.shape[0] // q_dev)
    lanes += -lanes % 128
    coded = jnp.pad(coded, (0, q_dev * lanes - coded.shape[0])).reshape(q_dev, lanes)
    packet = jnp.concatenate([queries, coded], axis=1)
    libs = [jnp.pad(lib, ((0, 0), (0, lanes))) for lib in (library, pair_lib)]
    lib_sqs = [jnp.sum(jnp.square(lib.astype(jnp.float32)), axis=1) for lib in (library, pair_lib)]
    got, parts = gather_rounds(
        packet, "blk", groups, lambda piece: piece_weights(piece, libs, lib_sqs, feat)
    )
    stats = join3(got[:, :, feat:].reshape(lineage, q_dev * lanes), 2 * width)
    stats = jnp.sum(stats, axis=0)
    stats = stats + swap(stats, "blk", core)

    col_sum, col_sq = stats[:width], stats[width:]
    total = library.shape[0] * nblk
    mean = col_sum / total
    spread = col_sq / total - mean * mean
    scale = lax.rsqrt(spread + EPS)
    numer = 0.0
    for k, vals in enumerate((values, pair_values)):
        zvals = ((vals - mean) * scale).astype(jnp.bfloat16)
        weight_b = jnp.concatenate([p[0][k] for p in parts], axis=0)
        numer = numer + jnp.dot(weight_b, zvals, preferred_element_type=jnp.float32)
    denom = jnp.concatenate([p[1] for p in parts], axis=0)
    den = jnp.broadcast_to(denom[:, None], (denom.shape[0], 128))
    sums = jnp.concatenate([numer, den], axis=1).reshape(lineage, q_dev, width + 128)
    sums = sums.reshape(tuple(len(offsets(g)) for g in groups) + sums.shape[1:])
    order = list(range(1, len(groups))) + [0]
    sums = jnp.transpose(sums, order + list(range(len(groups), sums.ndim)))
    mine = scatter_rounds(sums, "blk", [groups[k] for k in order])
    return mine[:, :width] / mine[:, width:width + 1]


def solution(mesh):
    return jax.shard_map(
        shards,
        mesh=mesh,
        in_specs=(P(("grp", "blk"), None), P(("grp", "blk"), None), P(("grp", "blk"), None)),
        out_specs=P(("grp", "blk"), None),
        check_vma=False,
    )
```

```python
import jax
import jax.numpy as jnp
from jax import lax
from jax.sharding import PartitionSpec as P

EPS = 1e-05
TAU = 0.05


def split3(x):
    hi = lax.reduce_precision(x, exponent_bits=8, mantissa_bits=7)
    rest = x - hi
    mid = lax.reduce_precision(rest, exponent_bits=8, mantissa_bits=7)
    lo = rest - mid
    return jnp.concatenate([hi, mid, lo], axis=-1).astype(jnp.bfloat16)


def join3(parts, n):
    parts = parts.astype(jnp.float32)
    return (parts[..., :n] + parts[..., n:2 * n]) + parts[..., 2 * n:3 * n]


def piece_weights(piece, libs, lib_sqs, feat):
    rows = piece.reshape(-1, piece.shape[-1])
    blockf = rows[:, :feat].astype(jnp.float32)
    q_sq = jnp.sum(blockf * blockf, axis=1)
    out, denom = [], 0.0
    for lib_ext, lib_sq in zip(libs, lib_sqs):
        inner = lax.dot_general(
            rows, lib_ext, (((1,), (1,)), ((), ())), preferred_element_type=jnp.float32
        )
        tanimoto = inner / (q_sq[:, None] + lib_sq[None, :] - inner)
        weight = jnp.exp((tanimoto - 1.0) / TAU)
        out.append(weight.astype(jnp.bfloat16))
        denom = denom + jnp.sum(weight, axis=1)
    return out, denom


def swap(x, axis, mask):
    count = lax.axis_size(axis)
    return lax.ppermute(x, axis, [(i, i ^ mask) for i in range(count)])


def digit_groups(count):
    bits = []
    while (1 << len(bits)) < count:
        bits.append(1 << len(bits))
    assert (1 << len(bits)) == count
    groups = [bits[:1], bits[1:2]]
    rest = bits[2:]
    while rest:
        groups.insert(2, rest[-2:])
        rest = rest[:-2]
    return [g for g in groups if g]


def offsets(group):
    masks = [0]
    for bit in group:
        masks = masks + [m | bit for m in masks]
    return masks


def cat(parts):
    return jnp.concatenate(parts, axis=0) if len(parts) > 1 else parts[0]


def gather_rounds(packet, axis, groups, work):
    rounds = list(reversed(groups))
    pieces = [packet[None]]
    results = []
    fresh = [packet[None]]
    early, mark = None, 0
    for r, group in enumerate(rounds):
        masks = offsets(group)[1:]
        if early is None:
            got = [[swap(cat(pieces), axis, m)] for m in masks]
        else:
            rest = cat(pieces[mark:])
            got = [[head, swap(rest, axis, m)] for head, m in zip(early, masks)]
        if r + 1 < len(rounds):
            early = [swap(cat(pieces), axis, m) for m in offsets(rounds[r + 1])[1:]]
            mark = len(pieces)
        if results:
            got, results[-1] = lax.optimization_barrier((got, results[-1]))
        got = [piece for pair in got for piece in pair]
        pieces += got
        fresh += got
        results.append(work(cat(fresh)))
        fresh = []
    return cat(pieces), results


def scatter_rounds(buf, axis, groups):
    for group in groups:
        masks = offsets(group)
        total = buf[0]
        for k in range(1, len(masks)):
            total = total + swap(buf[k], axis, masks[k])
        buf = total
    return buf


def shards(queries, library, assays):
    nblk = lax.axis_size("blk")
    groups = digit_groups(nblk)
    core, groups = groups[0][0], groups[1:]
    lineage = nblk // 2
    q_dev, feat = queries.shape
    width = assays.shape[1]
    values = assays.astype(jnp.float32)
    partial = jnp.concatenate([jnp.sum(values, axis=0), jnp.sum(values * values, axis=0)])

    pair_lib = swap(library, "blk", core)
    pair_values = swap(assays, "blk", core).astype(jnp.float32)

    coded = split3(partial)
    lanes = -(-coded.shape[0] // q_dev)
    lanes += -lanes % 128
    coded = jnp.pad(coded, (0, q_dev * lanes - coded.shape[0])).reshape(q_dev, lanes)
    packet = jnp.concatenate([queries, coded], axis=1)
    pair_lib, pair_values = lax.optimization_barrier((pair_lib, pair_values))
    libs = [jnp.pad(lib, ((0, 0), (0, lanes))) for lib in (library, pair_lib)]
    lib_sqs = [jnp.sum(jnp.square(lib.astype(jnp.float32)), axis=1) for lib in (library, pair_lib)]
    got, parts = gather_rounds(
        packet, "blk", groups, lambda piece: piece_weights(piece, libs, lib_sqs, feat)
    )
    stats = join3(got[:, :, feat:].reshape(lineage, q_dev * lanes), 2 * width)
    stats = jnp.sum(stats, axis=0)
    stats = stats + swap(stats, "blk", core)

    col_sum, col_sq = stats[:width], stats[width:]
    total = library.shape[0] * nblk
    mean = col_sum / total
    spread = col_sq / total - mean * mean
    scale = lax.rsqrt(spread + EPS)
    numer = 0.0
    for k, vals in enumerate((values, pair_values)):
        zvals = ((vals - mean) * scale).astype(jnp.bfloat16)
        weight_b = jnp.concatenate([p[0][k] for p in parts], axis=0)
        numer = numer + jnp.dot(weight_b, zvals, preferred_element_type=jnp.float32)
    denom = jnp.concatenate([p[1] for p in parts], axis=0)
    den = jnp.broadcast_to(denom[:, None], (denom.shape[0], 128))
    sums = jnp.concatenate([numer, den], axis=1).reshape(lineage, q_dev, width + 128)
    sums = sums.reshape(tuple(len(offsets(g)) for g in groups) + sums.shape[1:])
    order = list(range(1, len(groups))) + [0]
    sums = jnp.transpose(sums, order + list(range(len(groups), sums.ndim)))
    mine = scatter_rounds(sums, "blk", [groups[k] for k in order])
    return mine[:, :width] / mine[:, width:width + 1]


def solution(mesh):
    return jax.shard_map(
        shards,
        mesh=mesh,
        in_specs=(P(("grp", "blk"), None), P(("grp", "blk"), None), P(("grp", "blk"), None)),
        out_specs=P(("grp", "blk"), None),
        check_vma=False,
    )
```

```python
import jax
import jax.numpy as jnp
from jax import lax
from jax.sharding import PartitionSpec as P

EPS = 1e-05
TAU = 0.05


def split3(x):
    hi = lax.reduce_precision(x, exponent_bits=8, mantissa_bits=7)
    rest = x - hi
    mid = lax.reduce_precision(rest, exponent_bits=8, mantissa_bits=7)
    lo = rest - mid
    return jnp.concatenate([hi, mid, lo], axis=-1).astype(jnp.bfloat16)


def join3(parts, n):
    parts = parts.astype(jnp.float32)
    return (parts[..., :n] + parts[..., n:2 * n]) + parts[..., 2 * n:3 * n]


def piece_weights(piece, libs, lib_sqs, feat):
    rows = piece.reshape(-1, piece.shape[-1])
    blockf = rows[:, :feat].astype(jnp.float32)
    q_sq = jnp.sum(blockf * blockf, axis=1)
    out, denom = [], 0.0
    for lib_ext, lib_sq in zip(libs, lib_sqs):
        inner = lax.dot_general(
            rows, lib_ext, (((1,), (1,)), ((), ())), preferred_element_type=jnp.float32
        )
        tanimoto = inner / (q_sq[:, None] + lib_sq[None, :] - inner)
        weight = jnp.exp((tanimoto - 1.0) / TAU)
        out.append(weight.astype(jnp.bfloat16))
        denom = denom + jnp.sum(weight, axis=1)
    return out, denom


def swap(x, axis, mask):
    count = lax.axis_size(axis)
    return lax.ppermute(x, axis, [(i, i ^ mask) for i in range(count)])


def digit_groups(count):
    bits = []
    while (1 << len(bits)) < count:
        bits.append(1 << len(bits))
    assert (1 << len(bits)) == count
    groups = [bits[:1], bits[1:2]]
    rest = bits[2:]
    while rest:
        groups.insert(2, rest[-2:])
        rest = rest[:-2]
    return [g for g in groups if g]


def offsets(group):
    masks = [0]
    for bit in group:
        masks = masks + [m | bit for m in masks]
    return masks


def cat(parts):
    return jnp.concatenate(parts, axis=0) if len(parts) > 1 else parts[0]


def gather_rounds(packet, axis, groups, work):
    rounds = list(reversed(groups))
    pieces = [packet[None]]
    results = []
    fresh = [packet[None]]
    early, mark = None, 0
    for r, group in enumerate(rounds):
        masks = offsets(group)[1:]
        if early is None:
            got = [[swap(cat(pieces), axis, m)] for m in masks]
        else:
            rest = cat(pieces[mark:])
            got = [[head, swap(rest, axis, m)] for head, m in zip(early, masks)]
        if r + 1 < len(rounds):
            early = [swap(cat(pieces), axis, m) for m in offsets(rounds[r + 1])[1:]]
            mark = len(pieces)
        if results:
            got, results[-1] = lax.optimization_barrier((got, results[-1]))
        got = [piece for pair in got for piece in pair]
        pieces += got
        fresh += got
        results.append(work(cat(fresh)))
        fresh = []
    return cat(pieces), results


def scatter_rounds(buf, axis, groups):
    for group in groups:
        masks = offsets(group)
        total = buf[0]
        for k in range(1, len(masks)):
            total = total + swap(buf[k], axis, masks[k])
        buf = total
    return buf


def shards(queries, library, assays):
    nblk = lax.axis_size("blk")
    groups = digit_groups(nblk)
    core, groups = groups[0][0], groups[1:]
    lineage = nblk // 2
    q_dev, feat = queries.shape
    width = assays.shape[1]
    values = assays.astype(jnp.float32)
    partial = jnp.concatenate([jnp.sum(values, axis=0), jnp.sum(values * values, axis=0)])

    pair_lib = swap(library, "blk", core)
    pair_values = swap(assays, "blk", core).astype(jnp.float32)

    coded = split3(partial)
    lanes = -(-coded.shape[0] // q_dev)
    lanes += -lanes % 128
    coded = jnp.pad(coded, (0, q_dev * lanes - coded.shape[0])).reshape(q_dev, lanes)
    packet = jnp.concatenate([queries, coded], axis=1)
    libs = [jnp.pad(lib, ((0, 0), (0, lanes))) for lib in (library, pair_lib)]
    lib_sqs = [jnp.sum(jnp.square(lib.astype(jnp.float32)), axis=1) for lib in (library, pair_lib)]
    got, parts = gather_rounds(
        packet, "blk", groups, lambda piece: piece_weights(piece, libs, lib_sqs, feat)
    )
    stats = join3(got[:, :, feat:].reshape(lineage, q_dev * lanes), 2 * width)
    stats = jnp.sum(stats, axis=0)
    stats = stats + swap(stats, "blk", core)

    col_sum, col_sq = stats[:width], stats[width:]
    total = library.shape[0] * nblk
    mean = col_sum / total
    spread = col_sq / total - mean * mean
    scale = lax.rsqrt(spread + EPS)
    numer = 0.0
    for k, vals in enumerate((values, pair_values)):
        zvals = ((vals - mean) * scale).astype(jnp.bfloat16)
        weight_b = jnp.concatenate([p[0][k] for p in parts], axis=0)
        numer = numer + jnp.dot(weight_b, zvals, preferred_element_type=jnp.float32)
    denom = jnp.concatenate([p[1] for p in parts], axis=0)
    den = jnp.broadcast_to(denom[:, None], (denom.shape[0], width))
    sums = jnp.concatenate([numer, den], axis=1).reshape(lineage, q_dev, 2 * width)
    sums = sums.reshape(tuple(len(offsets(g)) for g in groups) + sums.shape[1:])
    order = list(range(1, len(groups))) + [0]
    sums = jnp.transpose(sums, order + list(range(len(groups), sums.ndim)))
    mine = scatter_rounds(sums, "blk", [groups[k] for k in order])
    return mine[:, :width] / mine[:, width:]


def solution(mesh):
    return jax.shard_map(
        shards,
        mesh=mesh,
        in_specs=(P(("grp", "blk"), None), P(("grp", "blk"), None), P(("grp", "blk"), None)),
        out_specs=P(("grp", "blk"), None),
        check_vma=False,
    )
```
